32 devices in a mesh: segment: 4 (over y, x), dom: 4 (over z), dp: 2 (over core).
Axes of the slice: x: 2, y: 2, z: 4, core: 2. Of those that a mesh axis runs over, the one named last changes fastest.
Arguments:
- node_in: bfloat16 [4, 512, 512], P('dp', 'dom'), may hold values from -6 to 6
- edge_in: bfloat16 [4, 512, 512], P('dp', 'dom'), may hold values from -6 to 6
- node_cot: bfloat16 [4, 512, 512], P('dp', 'dom'), may hold values from -6 to 6
- edge_cot: bfloat16 [4, 512, 512], P('dp', 'dom'), may hold values from -6 to 6
- send_rows: int32 [512], P('dom'), may hold values from 0 to 127
- sender_row: int32 [512], P('dom'), may hold values from 0 to 255
- receiver_row: int32 [512], P('dom'), may hold values from 0 to 127
- edge_count: int32 [4], P('dom'), may hold values from 1 to 128, 384 in all
- edge_w1: bfloat16 [4, 1536, 512], P('segment'), may hold values from -0.15625 to 0.15625
- edge_w2: bfloat16 [4, 512, 512], P('segment'), may hold values from -0.25 to 0.25
- node_w1: bfloat16 [4, 1024, 512], P('segment'), may hold values from -0.1875 to 0.1875
- node_w2: bfloat16 [4, 512, 512], P('segment'), may hold values from -0.25 to 0.25
- vectors: bfloat16 [4, 8, 512], P('segment'), may hold values from -2 to 2, as said below
Outputs:
- node_out: bfloat16 [4, 4, 512, 512], P('segment', 'dp', 'dom')
- edge_out: bfloat16 [4, 4, 512, 512], P('segment', 'dp', 'dom')
- node_grad: float32 [4, 4, 512, 512], P('segment', 'dp', 'dom')
- edge_grad: float32 [4, 4, 512, 512], P('segment', 'dp', 'dom')
- grad_edge_w1: float32 [4, 1536, 512], P('segment', None, ('dom', 'dp'))
- grad_edge_w2: float32 [4, 512, 512], P('segment', None, ('dom', 'dp'))
- grad_node_w1: float32 [4, 1024, 512], P('segment', None, ('dom', 'dp'))
- grad_node_w2: float32 [4, 512, 512], P('segment', None, ('dom', 'dp'))
- grad_vectors: float32 [4, 8, 512], P('segment', None, ('dom', 'dp'))
The draws below stay inside these ranges and needn't reach their ends.
Inputs may be any that keep to these rules, and one draw needn't show every extreme that they name: `vectors`: the parameter rows 2 and 6 of each layer are norm gains between 0.5 and 1.5, the others offsets. `edge_count`: one partition has all 128 slots live.
All inputs are finite; a program needn't handle non-finite values. No bound on the sum of `edge_count` on one device may be relied on, other than what follows from the above.
Results may differ from the reference program's by a relative error of at most 0.02.
Values may be sent and summed in bfloat16 or wider, within the bound.
No kernel may reach another device: no remote copies, remote signals or barrier semaphores. Data moves between devices by JAX's collectives and lax.ppermute only.
A program may use at most 128 MiB of HBM per device.

```python
import math
import jax
import jax.numpy as jnp
import numpy as np
from jax import lax

D = 512
NODE_DEV = 128
HALO = 64
EDGE_DEV = 128
LAYERS = 4
PARTITIONS = 4
NODES = 512
EDGES = 512
SAMPLES = 4
SENDS = 512


def draw_vectors(key, part):
    normal_key, uniform_key = jax.random.split(key)
    offsets = jnp.clip(0.5 * jax.random.normal(normal_key, (LAYERS, 8, D), jnp.float32), -2.0, 2.0)
    gains = jax.random.uniform(uniform_key, (LAYERS, 8, D), jnp.float32, 0.5, 1.5)
    row_ids = jnp.arange(8, dtype=jnp.int32)
    gain_rows = ((row_ids == 2) | (row_ids == 6))[None, :, None]
    return jnp.where(gain_rows, gains, offsets).astype(jnp.bfloat16)


def with_ends(drawn, own_key, least, largest):
    dims = drawn.shape
    index_at = [jax.random.randint(jax.random.fold_in(own_key, axis), (), 0, dims[axis]) for axis in range(len(dims))]
    drawn = drawn.at[tuple(index_at)].set(least)
    longest = dims.index(max(dims))
    index_at[longest] = (index_at[longest] + 1) % dims[longest]
    return drawn.at[tuple(index_at)].set(largest)


def raised(entries, own_key, source, target, blocks, factor):
    owner, partner = [(jnp.arange(entries.shape[axis_at]) // (entries.shape[axis_at] // blocks)).reshape([-1 if axis == axis_at else 1 for axis in range(entries.ndim)]) for axis_at in (source, target)]
    chosen = jax.random.permutation(own_key, blocks)[partner]
    strong = (owner == chosen) | (owner == (partner + blocks // 2) % blocks)
    return jnp.where(strong, factor * entries, entries)


def levels(own_key, extent, cuts, smallest, high):
    def one(axis_at, parts):
        heights = jax.random.uniform(jax.random.fold_in(jax.random.fold_in(own_key, 6), axis_at), (parts,), jnp.float32, smallest / len(cuts), high / len(cuts))
        return jnp.repeat(jnp.exp(heights), extent[axis_at] // parts).reshape((-1,) + (1,) * (len(extent) - axis_at - 1))

    loudness = one(*cuts[0])
    for cut in cuts[1:]:
        loudness = loudness * one(*cut)
    return loudness


def split_up(amount, total, limit, lean):
    loads = [(1 << 20) // math.isqrt(standing ** lean) + 1 for standing in range(2, amount + 1)]
    rest, holding = total - limit - (amount - 1), [1] * (amount - 1)
    while rest > 0:
        movable = [i for i in range(amount - 1) if holding[i] < limit]
        pool, budget = sum([loads[i] for i in movable]), rest
        for i in movable:
            extra = min(limit - holding[i], max(1, budget * loads[i] // pool), rest)
            holding[i] = holding[i] + extra
            rest = rest - extra
    return np.array([limit] + holding)


def uneven_parts(rng, amount, total, limit, lean):
    if amount == 2:
        one = jax.random.randint(rng, (), max(1, total - limit), min(limit, total - 1) + 1)
        return jnp.stack([one, total - one])
    sizes = jnp.asarray(split_up(amount, total, limit, lean), jnp.int32)
    twos = (amount - 1) // 2
    giver, receiver = sizes[1:1 + 2 * twos:2], sizes[2:2 + 2 * twos:2]
    room = jnp.minimum(giver - 1, limit - receiver)
    moved = jax.random.randint(jax.random.fold_in(rng, 1), (twos,), 0, 1 << 20) % (room + 1)
    sizes = sizes.at[1:1 + 2 * twos:2].set(giver - moved).at[2:2 + 2 * twos:2].set(receiver + moved)
    return sizes[jax.random.permutation(jax.random.fold_in(rng, 2), amount)]


def bell_draw(stream_key, dims, width, reach, cuts=(), kind=jnp.bfloat16):
    result = width * jax.random.normal(stream_key, dims, jnp.float32)
    if cuts:
        result = result * levels(stream_key, dims, cuts, -0.22, 0.18)
    return jnp.clip(result, -reach, reach).astype(kind)


def bell_draw_with(key, extent, deviation, most, cuts, heavy, kind=jnp.bfloat16):
    drawn = deviation * jax.random.normal(key, extent, jnp.float32)
    if cuts:
        drawn = drawn * levels(key, extent, cuts, -0.22, 0.18)
    return jnp.clip(raised(drawn, jax.random.fold_in(key, 3), *heavy), -most, most).astype(kind)


def setup_inputs(seed: int = 0) -> dict:
    key_of = jax.random.split(jax.random.key(seed), 14)
    return {
        "node_in": bell_draw(key_of[0], (SAMPLES, NODES, D), 1.0, 6.0, ((0, 2), (1, 4))),
        "edge_in": bell_draw(key_of[1], (SAMPLES, EDGES, D), 1.0, 6.0, ((0, 2), (1, 4))),
        "node_cot": bell_draw_with(key_of[2], (SAMPLES, NODES, D), 1.0, 6.0, ((0, 2), (1, 4)), (1, 2, 4, 2.0)),
        "edge_cot": bell_draw(key_of[3], (SAMPLES, EDGES, D), 1.0, 6.0, ((0, 2), (1, 4))),
        "send_rows": with_ends(jax.random.randint(key_of[4], (SENDS,), 0, NODE_DEV), jax.random.fold_in(key_of[4], 1), 0, NODE_DEV - 1).astype(jnp.int32),
        "sender_row": with_ends(jax.random.randint(key_of[5], (EDGES,), 0, NODE_DEV + 2 * HALO), jax.random.fold_in(key_of[5], 1), 0, (NODE_DEV + 2 * HALO) - 1).astype(jnp.int32),
        "receiver_row": with_ends(jax.random.randint(key_of[6], (EDGES,), 0, NODE_DEV), jax.random.fold_in(key_of[6], 1), 0, NODE_DEV - 1).astype(jnp.int32),
        "edge_count": uneven_parts(key_of[7], PARTITIONS, PARTITIONS * EDGE_DEV * 3 // 4, EDGE_DEV, 2).astype(jnp.int32),
        "edge_w1": bell_draw(key_of[8], (LAYERS, 3 * D, D), (3 * D) ** -0.5, 0.15625, ((0, 4),)),
        "edge_w2": bell_draw(key_of[9], (LAYERS, D, D), D ** -0.5, 0.25, ((0, 4),)),
        "node_w1": bell_draw(key_of[10], (LAYERS, 2 * D, D), (2 * D) ** -0.5, 0.1875, ((0, 4),)),
        "node_w2": bell_draw(key_of[11], (LAYERS, D, D), D ** -0.5, 0.25, ((0, 4),)),
        "vectors": draw_vectors(jax.random.fold_in(key_of[13], 71), 0),
    }


def layer_norm(values):
    average = lax.optimization_barrier(jnp.mean(values, -1, keepdims=True))
    centred = values - average
    return centred * lax.rsqrt(lax.optimization_barrier(jnp.mean(centred * centred, -1, keepdims=True)) + 1e-05)

def layer_local(node_rows, halo_rows, edge_rows, probes, weights, graph_lists):
    edge_w1, edge_w2, node_w1, node_w2, vectors = weights
    sender_row, receiver_row, live_mask = graph_lists
    coeffs = vectors.astype(jnp.float32)
    node_half = node_rows.astype(jnp.bfloat16)
    node_table = jnp.concatenate([node_half, halo_rows.astype(jnp.bfloat16)], 0)
    pick_send = (sender_row[:, None] == jnp.arange(node_table.shape[0], dtype=jnp.int32)[None, :]).astype(jnp.bfloat16)
    pick_recv = (receiver_row[:, None] == jnp.arange(node_rows.shape[0], dtype=jnp.int32)[None, :]).astype(jnp.bfloat16)
    senders = jnp.dot(pick_send, node_table, preferred_element_type=jnp.float32).astype(jnp.bfloat16)
    receivers = jnp.dot(pick_recv, node_half, preferred_element_type=jnp.float32).astype(jnp.bfloat16)
    joined = jnp.concatenate([edge_rows.astype(jnp.bfloat16), senders, receivers], 1)
    edge_pre = jnp.dot(joined, edge_w1, preferred_element_type=jnp.float32) + coeffs[0] + probes[0]
    edge_hid = jax.nn.silu(edge_pre).astype(jnp.bfloat16)
    edge_lin = jnp.dot(edge_hid, edge_w2, preferred_element_type=jnp.float32) + coeffs[1] + probes[1]
    edge_norm = layer_norm(edge_lin)
    message = (edge_norm * coeffs[2] + coeffs[3] + probes[2]) * live_mask[:, None]
    edge_next = edge_rows + message
    incoming = lax.dot_general(pick_recv, message.astype(jnp.bfloat16), (((0,), (0,)), ((), ())), preferred_element_type=jnp.float32)
    node_cat = jnp.concatenate([node_half, incoming.astype(jnp.bfloat16)], 1)
    node_pre = jnp.dot(node_cat, node_w1, preferred_element_type=jnp.float32) + coeffs[4] + probes[3]
    node_hid = jax.nn.silu(node_pre).astype(jnp.bfloat16)
    node_lin = jnp.dot(node_hid, node_w2, preferred_element_type=jnp.float32) + coeffs[5] + probes[4]
    node_norm = layer_norm(node_lin)
    node_next = node_rows + node_norm * coeffs[6] + coeffs[7] + probes[5]
    return ((node_next, edge_next), (joined, edge_hid, edge_norm, node_cat, node_hid, node_norm))

def blank_probes(node_count, edge_total, features):
    edge_zero = jnp.zeros((edge_total, features), jnp.float32)
    node_zero = jnp.zeros((node_count, features), jnp.float32)
    return (edge_zero, edge_zero, edge_zero, node_zero, node_zero, node_zero)

def transposed(left, cotangent):
    return lax.dot_general(left, cotangent.astype(jnp.bfloat16), (((0,), (0,)), ((), ())), preferred_element_type=jnp.float32)

def weight_grads(saved, probe_back):
    joined, edge_hid, edge_norm, node_cat, node_hid, node_norm = saved
    edge_pre_back, edge_lin_back, message_back, node_pre_back, node_lin_back, node_out_back = probe_back
    vector_back = jnp.stack([edge_pre_back.sum(0), edge_lin_back.sum(0), (message_back * edge_norm).sum(0), message_back.sum(0), node_pre_back.sum(0), node_lin_back.sum(0), (node_out_back * node_norm).sum(0), node_out_back.sum(0)], 0)
    return (transposed(joined, edge_pre_back), transposed(edge_hid, edge_lin_back), transposed(node_cat, node_pre_back), transposed(node_hid, node_lin_back), vector_back)

def forward_one(node_half, halo_half, edge_half, graph_lists, weights):
    probes = blank_probes(node_half.shape[0], edge_half.shape[0], node_half.shape[1])
    results, saved = layer_local(node_half.astype(jnp.float32), halo_half.astype(jnp.float32), edge_half.astype(jnp.float32), probes, weights, graph_lists)
    return (results[0].astype(jnp.bfloat16), results[1].astype(jnp.bfloat16))

def backward_one(node_half, halo_half, edge_half, node_back, edge_back, graph_lists, weights):
    probes = blank_probes(node_half.shape[0], edge_half.shape[0], node_half.shape[1])

    def local_layer(node_rows, halo_rows, edge_rows, probe_rows):
        return layer_local(node_rows, halo_rows, edge_rows, probe_rows, weights, graph_lists)
    results, pullback, saved = jax.vjp(local_layer, node_half.astype(jnp.float32), halo_half.astype(jnp.float32), edge_half.astype(jnp.float32), probes, has_aux=True)
    node_grad_in, halo_grad, edge_grad_in, probe_back = pullback((node_back, edge_back))
    return (node_grad_in, halo_grad, edge_grad_in, weight_grads(saved, probe_back))

def halo_of(node_half, send_lists):
    outgoing = jax.vmap(jnp.take, in_axes=(0, 0, None))(node_half, send_lists, 0)
    return jnp.concatenate([jnp.roll(outgoing, 1, 0)[:, HALO:], jnp.roll(outgoing, -1, 0)[:, :HALO]], 1)

def returned_of(halo_back):
    return jnp.concatenate([jnp.roll(halo_back, 1, 0)[:, HALO:], jnp.roll(halo_back, -1, 0)[:, :HALO]], 1)

def scatter_rows(values, row_ids):
    return jnp.zeros((NODE_DEV, values.shape[1]), jnp.float32).at[row_ids].add(values)

def reference(node_in, edge_in, node_cot, edge_cot, send_rows, sender_row, receiver_row, edge_count, edge_w1, edge_w2, node_w1, node_w2, vectors):
    partitions = PARTITIONS
    send_lists = send_rows.reshape(partitions, 2 * HALO)
    live_mask = (jnp.arange(EDGE_DEV, dtype=jnp.int32)[None, :] < edge_count[:, None]).astype(jnp.float32)
    graph_lists = (sender_row.reshape(partitions, EDGE_DEV), receiver_row.reshape(partitions, EDGE_DEV), live_mask)
    forward_map = jax.vmap(forward_one, in_axes=(0, 0, 0, 0, None))
    backward_map = jax.vmap(backward_one, in_axes=(0, 0, 0, 0, 0, 0, None))
    node_outs = [[] for layer_index in range(LAYERS)]
    edge_outs = [[] for layer_index in range(LAYERS)]
    node_grads = [[] for layer_index in range(LAYERS)]
    edge_grads = [[] for layer_index in range(LAYERS)]
    grad_store = [None for layer_index in range(LAYERS)]
    for sample in range(SAMPLES):
        node_half = node_in[sample].reshape(partitions, NODE_DEV, D)
        edge_half = edge_in[sample].reshape(partitions, EDGE_DEV, D)
        stored = []
        for layer_index in range(LAYERS):
            weights = (edge_w1[layer_index], edge_w2[layer_index], node_w1[layer_index], node_w2[layer_index], vectors[layer_index])
            halo_half = halo_of(node_half, send_lists)
            stored.append((node_half, halo_half, edge_half))
            node_half, edge_half = forward_map(node_half, halo_half, edge_half, graph_lists, weights)
            node_outs[layer_index].append(node_half.reshape(NODES, D))
            edge_outs[layer_index].append(edge_half.reshape(EDGES, D))
        node_back = node_cot[sample].astype(jnp.float32).reshape(partitions, NODE_DEV, D)
        edge_back = edge_cot[sample].astype(jnp.float32).reshape(partitions, EDGE_DEV, D)
        for layer_index in reversed(range(LAYERS)):
            weights = (edge_w1[layer_index], edge_w2[layer_index], node_w1[layer_index], node_w2[layer_index], vectors[layer_index])
            node_saved, halo_saved, edge_saved = stored[layer_index]
            node_back, halo_back, edge_back, grads = backward_map(node_saved, halo_saved, edge_saved, node_back, edge_back, graph_lists, weights)
            node_back = node_back + jax.vmap(scatter_rows)(returned_of(halo_back), send_lists)
            node_grads[layer_index].append(node_back.reshape(NODES, D))
            edge_grads[layer_index].append(edge_back.reshape(EDGES, D))
            summed = tuple((lax.optimization_barrier(jnp.sum(value, 0)) for value in grads))
            if grad_store[layer_index] is None:
                grad_store[layer_index] = summed
            else:
                grad_store[layer_index] = tuple((first + second for first, second in zip(grad_store[layer_index], summed)))
    node_out = jnp.stack([jnp.stack(node_outs[layer_index]) for layer_index in range(LAYERS)])
    edge_out = jnp.stack([jnp.stack(edge_outs[layer_index]) for layer_index in range(LAYERS)])
    node_grad = jnp.stack([jnp.stack(node_grads[layer_index]) for layer_index in range(LAYERS)])
    edge_grad = jnp.stack([jnp.stack(edge_grads[layer_index]) for layer_index in range(LAYERS)])
    grad_edge_w1 = jnp.stack([grad_store[layer_index][0] for layer_index in range(LAYERS)])
    grad_edge_w2 = jnp.stack([grad_store[layer_index][1] for layer_index in range(LAYERS)])
    grad_node_w1 = jnp.stack([grad_store[layer_index][2] for layer_index in range(LAYERS)])
    grad_node_w2 = jnp.stack([grad_store[layer_index][3] for layer_index in range(LAYERS)])
    grad_vectors = jnp.stack([grad_store[layer_index][4] for layer_index in range(LAYERS)])
    return (node_out, edge_out, node_grad, edge_grad, grad_edge_w1, grad_edge_w2, grad_node_w1, grad_node_w2, grad_vectors)
```

```python
import jax
import jax.numpy as jnp
from jax import lax
from jax.sharding import PartitionSpec as P


def layer_norm(values):
    average = jnp.mean(values, -1, keepdims=True)
    centred = values - average
    return centred * lax.rsqrt(jnp.mean(centred * centred, -1, keepdims=True) + 1e-05)


def layer_local(node_rows, halo_rows, edge_rows, probes, weights, graph_lists):
    edge_w1, edge_w2, node_w1, node_w2, vectors = weights
    sender_row, receiver_row, live_mask = graph_lists
    coeffs = vectors.astype(jnp.float32)
    node_half = node_rows.astype(jnp.bfloat16)
    node_table = jnp.concatenate([node_half, halo_rows.astype(jnp.bfloat16)], 0)
    pick_send = (
        sender_row[:, None] == jnp.arange(node_table.shape[0], dtype=jnp.int32)[None, :]
    ).astype(jnp.bfloat16)
    pick_recv = (
        receiver_row[:, None] == jnp.arange(node_rows.shape[0], dtype=jnp.int32)[None, :]
    ).astype(jnp.bfloat16)
    senders = jnp.dot(pick_send, node_table, preferred_element_type=jnp.float32).astype(
        jnp.bfloat16
    )
    receivers = jnp.dot(pick_recv, node_half, preferred_element_type=jnp.float32).astype(
        jnp.bfloat16
    )
    joined = jnp.concatenate([edge_rows.astype(jnp.bfloat16), senders, receivers], 1)
    edge_pre = jnp.dot(joined, edge_w1, preferred_element_type=jnp.float32) + coeffs[0] + probes[0]
    edge_hid = jax.nn.silu(edge_pre).astype(jnp.bfloat16)
    edge_lin = (
        jnp.dot(edge_hid, edge_w2, preferred_element_type=jnp.float32) + coeffs[1] + probes[1]
    )
    edge_norm = layer_norm(edge_lin)
    message = (edge_norm * coeffs[2] + coeffs[3] + probes[2]) * live_mask[:, None]
    edge_next = edge_rows + message
    incoming = lax.dot_general(
        pick_recv,
        message.astype(jnp.bfloat16),
        (((0,), (0,)), ((), ())),
        preferred_element_type=jnp.float32,
    )
    node_cat = jnp.concatenate([node_half, incoming.astype(jnp.bfloat16)], 1)
    node_pre = (
        jnp.dot(node_cat, node_w1, preferred_element_type=jnp.float32) + coeffs[4] + probes[3]
    )
    node_hid = jax.nn.silu(node_pre).astype(jnp.bfloat16)
    node_lin = (
        jnp.dot(node_hid, node_w2, preferred_element_type=jnp.float32) + coeffs[5] + probes[4]
    )
    node_norm = layer_norm(node_lin)
    node_next = node_rows + node_norm * coeffs[6] + coeffs[7] + probes[5]
    return ((node_next, edge_next), (joined, edge_hid, edge_norm, node_cat, node_hid, node_norm))


def batched_layer(weights, graph_lists):

    def one(node_rows, halo_rows, edge_rows, probes):
        return layer_local(node_rows, halo_rows, edge_rows, probes, weights, graph_lists)

    return jax.vmap(one)


def transposed(left, cotangent):
    return lax.dot_general(
        left,
        cotangent.astype(jnp.bfloat16),
        (((0,), (0,)), ((), ())),
        preferred_element_type=jnp.float32,
    )


def weight_grads(saved, probe_back):
    joined, edge_hid, edge_norm, node_cat, node_hid, node_norm = saved
    edge_pre_back, edge_lin_back, message_back, node_pre_back, node_lin_back, node_out_back = (
        probe_back
    )
    vector_back = jnp.stack(
        [
            edge_pre_back.sum(0),
            edge_lin_back.sum(0),
            (message_back * edge_norm).sum(0),
            message_back.sum(0),
            node_pre_back.sum(0),
            node_lin_back.sum(0),
            (node_out_back * node_norm).sum(0),
            node_out_back.sum(0),
        ],
        0,
    )
    return (
        transposed(joined, edge_pre_back),
        transposed(edge_hid, edge_lin_back),
        transposed(node_cat, node_pre_back),
        transposed(node_hid, node_lin_back),
        vector_back,
    )


def flatten_rows(buffer):
    return buffer.reshape(-1, buffer.shape[-1])


def exchange(rows, margin):
    count = lax.axis_size("dom")
    from_prev = lax.ppermute(rows[:, margin:], "dom", [(i, (i + 1) % count) for i in range(count)])
    from_next = lax.ppermute(rows[:, :margin], "dom", [((i + 1) % count, i) for i in range(count)])
    return jnp.concatenate([from_prev, from_next], 1)


def gather_weights(params):
    shapes = [value.shape[1:] for value in params]
    packed = jnp.concatenate([value[0] for value in params], 0)
    share_count = lax.axis_size("dp")
    total = packed.shape[0]
    padded_total = -(-total // (8 * share_count)) * (8 * share_count)
    packed = jnp.pad(packed, ((0, padded_total - total), (0, 0)))
    share = padded_total // share_count
    piece = lax.dynamic_slice_in_dim(packed, lax.axis_index("dp") * share, share, 0)
    gathered = lax.all_gather(piece, ("segment", "dp"), axis=0, tiled=False)
    layer_count = gathered.shape[0] // share_count
    gathered = gathered.reshape(layer_count, padded_total, packed.shape[1])
    layers = []
    for layer_index in range(layer_count):
        start = 0
        parts = []
        for shape in shapes:
            parts.append(gathered[layer_index, start : start + shape[0]])
            start += shape[0]
        layers.append(tuple(parts))
    return layers


def reduce_layer_grads(totals):
    segment_count = lax.axis_size("segment")
    segment_index = lax.axis_index("segment")
    sizes = [value.shape[0] // segment_count for value in totals]
    blocks = [
        lax.dynamic_slice_in_dim(value, segment_index * size, size, 0)
        for value, size in zip(totals, sizes)
    ]
    packed = jnp.concatenate(blocks, 0)
    reduced = lax.psum_scatter(packed, ("dom", "dp"), scatter_dimension=1, tiled=True)
    gathered = lax.all_gather(reduced, "segment", axis=0, tiled=False)
    results = []
    start = 0
    for size in sizes:
        results.append(flatten_rows(gathered[:, start : start + size]))
        start += size
    return results


def local(
    node_in,
    edge_in,
    node_cot,
    edge_cot,
    send_rows,
    sender_row,
    receiver_row,
    edge_count,
    edge_w1,
    edge_w2,
    node_w1,
    node_w2,
    vectors,
):
    segment_index = lax.axis_index("segment")
    edge_total = edge_in.shape[1]
    margin = send_rows.shape[0] // 2
    live_mask = (jnp.arange(edge_total, dtype=jnp.int32) < edge_count[0]).astype(jnp.float32)
    graph_lists = (sender_row, receiver_row, live_mask)
    layers = gather_weights((edge_w1, edge_w2, node_w1, node_w2, vectors))
    edge_zero = jnp.zeros(edge_in.shape, jnp.float32)
    node_zero = jnp.zeros(node_in.shape, jnp.float32)
    probes = (edge_zero, edge_zero, edge_zero, node_zero, node_zero, node_zero)

    node_h = node_in
    edge_h = edge_in
    pullbacks = []
    node_outs = []
    edge_outs = []
    for weights in layers:
        halo_h = exchange(jnp.take(node_h, send_rows, axis=1), margin)
        (node_next, edge_next), pullback, saved = jax.vjp(
            batched_layer(weights, graph_lists),
            node_h.astype(jnp.float32),
            halo_h.astype(jnp.float32),
            edge_h.astype(jnp.float32),
            probes,
            has_aux=True,
        )
        pullbacks.append((pullback, saved))
        node_h = node_next.astype(jnp.bfloat16)
        edge_h = edge_next.astype(jnp.bfloat16)
        node_outs.append(node_h)
        edge_outs.append(edge_h)

    node_back = node_cot.astype(jnp.float32)
    edge_back = edge_cot.astype(jnp.float32)
    node_grads = [None] * len(layers)
    edge_grads = [None] * len(layers)
    grads = [None] * len(layers)
    for layer_index in reversed(range(len(layers))):
        pullback, saved = pullbacks[layer_index]
        node_back, halo_back, edge_back, probe_back = pullback((node_back, edge_back))
        returned = exchange(halo_back.astype(jnp.bfloat16), margin).astype(jnp.float32)
        node_back = node_back + jnp.zeros_like(node_back).at[:, send_rows].add(returned)
        node_grads[layer_index] = node_back
        edge_grads[layer_index] = edge_back
        totals = weight_grads(
            tuple(flatten_rows(value) for value in saved),
            tuple(flatten_rows(value) for value in probe_back),
        )
        grads[layer_index] = reduce_layer_grads(totals)

    def mine(values):
        return lax.dynamic_index_in_dim(jnp.stack(values), segment_index, 0, keepdims=True)

    return (
        mine(node_outs),
        mine(edge_outs),
        mine(node_grads),
        mine(edge_grads),
        mine([grad[0] for grad in grads]),
        mine([grad[1] for grad in grads]),
        mine([grad[2] for grad in grads]),
        mine([grad[3] for grad in grads]),
        mine([grad[4] for grad in grads]),
    )


def solution(mesh):
    in_specs = (
        P("dp", "dom", None),
        P("dp", "dom", None),
        P("dp", "dom", None),
        P("dp", "dom", None),
        P("dom"),
        P("dom"),
        P("dom"),
        P("dom"),
        P("segment", None, None),
        P("segment", None, None),
        P("segment", None, None),
        P("segment", None, None),
        P("segment", None, None),
    )
    out_specs = (
        P("segment", "dp", "dom", None),
        P("segment", "dp", "dom", None),
        P("segment", "dp", "dom", None),
        P("segment", "dp", "dom", None),
        P("segment", None, ("dom", "dp")),
        P("segment", None, ("dom", "dp")),
        P("segment", None, ("dom", "dp")),
        P("segment", None, ("dom", "dp")),
        P("segment", None, ("dom", "dp")),
    )
    return jax.shard_map(local, mesh=mesh, in_specs=in_specs, out_specs=out_specs, check_vma=False)
```

```python
import jax
import jax.numpy as jnp
from jax import lax
from jax.sharding import PartitionSpec as P


def layer_norm(values):
    average = jnp.mean(values, -1, keepdims=True)
    centred = values - average
    return centred * lax.rsqrt(jnp.mean(centred * centred, -1, keepdims=True) + 1e-05)


def layer_local(node_rows, halo_rows, edge_rows, probes, weights, graph_lists):
    edge_w1, edge_w2, node_w1, node_w2, vectors = weights
    sender_row, receiver_row, live_mask = graph_lists
    coeffs = vectors.astype(jnp.float32)
    node_half = node_rows.astype(jnp.bfloat16)
    node_table = jnp.concatenate([node_half, halo_rows.astype(jnp.bfloat16)], 0)
    pick_send = (
        sender_row[:, None] == jnp.arange(node_table.shape[0], dtype=jnp.int32)[None, :]
    ).astype(jnp.bfloat16)
    pick_recv = (
        receiver_row[:, None] == jnp.arange(node_rows.shape[0], dtype=jnp.int32)[None, :]
    ).astype(jnp.bfloat16)
    senders = jnp.dot(pick_send, node_table, preferred_element_type=jnp.float32).astype(
        jnp.bfloat16
    )
    receivers = jnp.dot(pick_recv, node_half, preferred_element_type=jnp.float32).astype(
        jnp.bfloat16
    )
    joined = jnp.concatenate([edge_rows.astype(jnp.bfloat16), senders, receivers], 1)
    edge_pre = jnp.dot(joined, edge_w1, preferred_element_type=jnp.float32) + coeffs[0] + probes[0]
    edge_hid = jax.nn.silu(edge_pre).astype(jnp.bfloat16)
    edge_lin = (
        jnp.dot(edge_hid, edge_w2, preferred_element_type=jnp.float32) + coeffs[1] + probes[1]
    )
    edge_norm = layer_norm(edge_lin)
    message = (edge_norm * coeffs[2] + coeffs[3] + probes[2]) * live_mask[:, None]
    edge_next = edge_rows + message
    incoming = lax.dot_general(
        pick_recv,
        message.astype(jnp.bfloat16),
        (((0,), (0,)), ((), ())),
        preferred_element_type=jnp.float32,
    )
    node_cat = jnp.concatenate([node_half, incoming.astype(jnp.bfloat16)], 1)
    node_pre = (
        jnp.dot(node_cat, node_w1, preferred_element_type=jnp.float32) + coeffs[4] + probes[3]
    )
    node_hid = jax.nn.silu(node_pre).astype(jnp.bfloat16)
    node_lin = (
        jnp.dot(node_hid, node_w2, preferred_element_type=jnp.float32) + coeffs[5] + probes[4]
    )
    node_norm = layer_norm(node_lin)
    node_next = node_rows + node_norm * coeffs[6] + coeffs[7] + probes[5]
    return ((node_next, edge_next), (joined, edge_hid, edge_norm, node_cat, node_hid, node_norm))


def batched_layer(weights, graph_lists):

    def one(node_rows, halo_rows, edge_rows, probes):
        return layer_local(node_rows, halo_rows, edge_rows, probes, weights, graph_lists)

    return jax.vmap(one)


def transposed(left, cotangent):
    return lax.dot_general(
        left,
        cotangent.astype(jnp.bfloat16),
        (((0,), (0,)), ((), ())),
        preferred_element_type=jnp.float32,
    )


def weight_grads(saved, probe_back):
    joined, edge_hid, edge_norm, node_cat, node_hid, node_norm = saved
    edge_pre_back, edge_lin_back, message_back, node_pre_back, node_lin_back, node_out_back = (
        probe_back
    )
    vector_back = jnp.stack(
        [
            edge_pre_back.sum(0),
            edge_lin_back.sum(0),
            (message_back * edge_norm).sum(0),
            message_back.sum(0),
            node_pre_back.sum(0),
            node_lin_back.sum(0),
            (node_out_back * node_norm).sum(0),
            node_out_back.sum(0),
        ],
        0,
    )
    return (
        transposed(joined, edge_pre_back),
        transposed(edge_hid, edge_lin_back),
        transposed(node_cat, node_pre_back),
        transposed(node_hid, node_lin_back),
        vector_back,
    )


def flatten_rows(buffer):
    return buffer.reshape(-1, buffer.shape[-1])


def exchange(rows, margin):
    count = lax.axis_size("dom")
    from_prev = lax.ppermute(rows[:, margin:], "dom", [(i, (i + 1) % count) for i in range(count)])
    from_next = lax.ppermute(rows[:, :margin], "dom", [((i + 1) % count, i) for i in range(count)])
    return jnp.concatenate([from_prev, from_next], 1)


def gather_weights(params):
    shapes = [value.shape[1:] for value in params]
    packed = jnp.concatenate([value[0] for value in params], 0)
    share_count = lax.axis_size("dp")
    total = packed.shape[0]
    padded_total = -(-total // (8 * share_count)) * (8 * share_count)
    packed = jnp.pad(packed, ((0, padded_total - total), (0, 0)))
    share = padded_total // share_count
    piece = lax.dynamic_slice_in_dim(packed, lax.axis_index("dp") * share, share, 0)
    gathered = lax.all_gather(piece, ("segment", "dp"), axis=0, tiled=False)
    layer_count = gathered.shape[0] // share_count
    gathered = gathered.reshape(layer_count, padded_total, packed.shape[1])
    layers = []
    for layer_index in range(layer_count):
        start = 0
        parts = []
        for shape in shapes:
            parts.append(gathered[layer_index, start : start + shape[0]])
            start += shape[0]
        layers.append(tuple(parts))
    return layers


def reduce_layer_grads(totals):
    segment_count = lax.axis_size("segment")
    segment_index = lax.axis_index("segment")
    sizes = [value.shape[0] // segment_count for value in totals]
    blocks = [
        lax.dynamic_slice_in_dim(value, segment_index * size, size, 0)
        for value, size in zip(totals, sizes)
    ]
    packed = jnp.concatenate(blocks, 0)
    return lax.psum_scatter(packed, ("dom", "dp"), scatter_dimension=1, tiled=True), sizes


def own_layer_grads(reduced, sizes):
    exchanged = lax.all_to_all(jnp.stack(reduced), "segment", 0, 0, tiled=True)
    results = []
    start = 0
    for size in sizes:
        results.append(flatten_rows(exchanged[:, start : start + size])[None])
        start += size
    return results


def local(
    node_in,
    edge_in,
    node_cot,
    edge_cot,
    send_rows,
    sender_row,
    receiver_row,
    edge_count,
    edge_w1,
    edge_w2,
    node_w1,
    node_w2,
    vectors,
):
    segment_index = lax.axis_index("segment")
    edge_total = edge_in.shape[1]
    margin = send_rows.shape[0] // 2
    live_mask = (jnp.arange(edge_total, dtype=jnp.int32) < edge_count[0]).astype(jnp.float32)
    graph_lists = (sender_row, receiver_row, live_mask)
    layers = gather_weights((edge_w1, edge_w2, node_w1, node_w2, vectors))
    edge_zero = jnp.zeros(edge_in.shape, jnp.float32)
    node_zero = jnp.zeros(node_in.shape, jnp.float32)
    probes = (edge_zero, edge_zero, edge_zero, node_zero, node_zero, node_zero)
    pick_sent = (
        send_rows[:, None] == jnp.arange(node_in.shape[1], dtype=jnp.int32)[None, :]
    ).astype(jnp.bfloat16)

    node_h = node_in
    edge_h = edge_in
    pullbacks = []
    node_outs = []
    edge_outs = []
    for weights in layers:
        halo_h = exchange(jnp.take(node_h, send_rows, axis=1), margin)
        (node_next, edge_next), pullback, saved = jax.vjp(
            batched_layer(weights, graph_lists),
            node_h.astype(jnp.float32),
            halo_h.astype(jnp.float32),
            edge_h.astype(jnp.float32),
            probes,
            has_aux=True,
        )
        pullbacks.append((pullback, saved))
        node_h = node_next.astype(jnp.bfloat16)
        edge_h = edge_next.astype(jnp.bfloat16)
        node_outs.append(node_h)
        edge_outs.append(edge_h)

    node_back = node_cot.astype(jnp.float32)
    edge_back = edge_cot.astype(jnp.float32)
    node_grads = [None] * len(layers)
    edge_grads = [None] * len(layers)
    grads = [None] * len(layers)
    for layer_index in reversed(range(len(layers))):
        pullback, saved = pullbacks[layer_index]
        node_back, halo_back, edge_back, probe_back = pullback((node_back, edge_back))
        returned = exchange(halo_back.astype(jnp.bfloat16), margin)
        node_back = node_back + jnp.einsum(
            "kn,skd->snd", pick_sent, returned, preferred_element_type=jnp.float32
        )
        node_grads[layer_index] = node_back
        edge_grads[layer_index] = edge_back
        totals = weight_grads(
            tuple(flatten_rows(value) for value in saved),
            tuple(flatten_rows(value) for value in probe_back),
        )
        grads[layer_index], sizes = reduce_layer_grads(totals)
    own = own_layer_grads(grads, sizes)

    def mine(values):
        return lax.dynamic_index_in_dim(jnp.stack(values), segment_index, 0, keepdims=True)

    return (
        mine(node_outs),
        mine(edge_outs),
        mine(node_grads),
        mine(edge_grads),
        own[0],
        own[1],
        own[2],
        own[3],
        own[4],
    )


def solution(mesh):
    in_specs = (
        P("dp", "dom", None),
        P("dp", "dom", None),
        P("dp", "dom", None),
        P("dp", "dom", None),
        P("dom"),
        P("dom"),
        P("dom"),
        P("dom"),
        P("segment", None, None),
        P("segment", None, None),
        P("segment", None, None),
        P("segment", None, None),
        P("segment", None, None),
    )
    out_specs = (
        P("segment", "dp", "dom", None),
        P("segment", "dp", "dom", None),
        P("segment", "dp", "dom", None),
        P("segment", "dp", "dom", None),
        P("segment", None, ("dom", "dp")),
        P("segment", None, ("dom", "dp")),
        P("segment", None, ("dom", "dp")),
        P("segment", None, ("dom", "dp")),
        P("segment", None, ("dom", "dp")),
    )
    return jax.shard_map(local, mesh=mesh, in_specs=in_specs, out_specs=out_specs, check_vma=False)
```

```python
import jax
import jax.numpy as jnp
from jax import lax
from jax.sharding import PartitionSpec as P


def layer_norm(values):
    average = jnp.mean(values, -1, keepdims=True)
    centred = values - average
    return centred * lax.rsqrt(jnp.mean(centred * centred, -1, keepdims=True) + 1e-05)


def layer_local(node_rows, halo_rows, edge_rows, probes, weights, graph_lists):
    edge_w1, edge_w2, node_w1, node_w2, vectors = weights
    sender_row, receiver_row, live_mask = graph_lists
    coeffs = vectors.astype(jnp.float32)
    node_half = node_rows.astype(jnp.bfloat16)
    node_table = jnp.concatenate([node_half, halo_rows.astype(jnp.bfloat16)], 0)
    pick_send = (
        sender_row[:, None] == jnp.arange(node_table.shape[0], dtype=jnp.int32)[None, :]
    ).astype(jnp.bfloat16)
    pick_recv = (
        receiver_row[:, None] == jnp.arange(node_rows.shape[0], dtype=jnp.int32)[None, :]
    ).astype(jnp.bfloat16)
    senders = jnp.dot(pick_send, node_table, preferred_element_type=jnp.float32).astype(
        jnp.bfloat16
    )
    receivers = jnp.dot(pick_recv, node_half, preferred_element_type=jnp.float32).astype(
        jnp.bfloat16
    )
    joined = jnp.concatenate([edge_rows.astype(jnp.bfloat16), senders, receivers], 1)
    edge_pre = jnp.dot(joined, edge_w1, preferred_element_type=jnp.float32) + coeffs[0] + probes[0]
    edge_hid = jax.nn.silu(edge_pre).astype(jnp.bfloat16)
    edge_lin = (
        jnp.dot(edge_hid, edge_w2, preferred_element_type=jnp.float32) + coeffs[1] + probes[1]
    )
    edge_norm = layer_norm(edge_lin)
    message = (edge_norm * coeffs[2] + coeffs[3] + probes[2]) * live_mask[:, None]
    edge_next = edge_rows + message
    incoming = lax.dot_general(
        pick_recv,
        message.astype(jnp.bfloat16),
        (((0,), (0,)), ((), ())),
        preferred_element_type=jnp.float32,
    )
    node_cat = jnp.concatenate([node_half, incoming.astype(jnp.bfloat16)], 1)
    node_pre = (
        jnp.dot(node_cat, node_w1, preferred_element_type=jnp.float32) + coeffs[4] + probes[3]
    )
    node_hid = jax.nn.silu(node_pre).astype(jnp.bfloat16)
    node_lin = (
        jnp.dot(node_hid, node_w2, preferred_element_type=jnp.float32) + coeffs[5] + probes[4]
    )
    node_norm = layer_norm(node_lin)
    node_next = node_rows + node_norm * coeffs[6] + coeffs[7] + probes[5]
    return ((node_next, edge_next), (joined, edge_hid, edge_norm, node_cat, node_hid, node_norm))


def batched_layer(weights, graph_lists):

    def one(node_rows, halo_rows, edge_rows, probes):
        return layer_local(node_rows, halo_rows, edge_rows, probes, weights, graph_lists)

    return jax.vmap(one)


def flatten_rows(buffer):
    return buffer.reshape(-1, buffer.shape[-1])


def exchange(rows, margin):
    count = lax.axis_size("dom")
    from_prev = lax.ppermute(rows[:, margin:], "dom", [(i, (i + 1) % count) for i in range(count)])
    from_next = lax.ppermute(rows[:, :margin], "dom", [((i + 1) % count, i) for i in range(count)])
    return jnp.concatenate([from_prev, from_next], 1)


def gather_weights(params):
    shapes = [value.shape[1:] for value in params]
    packed = jnp.concatenate([value[0] for value in params], 0)
    share_count = lax.axis_size("dp")
    total = packed.shape[0]
    padded_total = -(-total // (8 * share_count)) * (8 * share_count)
    packed = jnp.pad(packed, ((0, padded_total - total), (0, 0)))
    share = padded_total // share_count
    piece = lax.dynamic_slice_in_dim(packed, lax.axis_index("dp") * share, share, 0)
    gathered = lax.all_gather(piece, ("segment", "dp"), axis=0, tiled=False)
    layer_count = gathered.shape[0] // share_count
    gathered = gathered.reshape(layer_count, padded_total, packed.shape[1])
    layers = []
    for layer_index in range(layer_count):
        start = 0
        parts = []
        for shape in shapes:
            parts.append(gathered[layer_index, start : start + shape[0]])
            start += shape[0]
        layers.append(tuple(parts))
    return layers


def layer_grad_block(saved, probe_back):
    segment_count = lax.axis_size("segment")
    segment_index = lax.axis_index("segment")
    joined, edge_hid, edge_norm, node_cat, node_hid, node_norm = saved
    edge_pre_back, edge_lin_back, message_back, node_pre_back, node_lin_back, node_out_back = (
        probe_back
    )
    parts = []
    for left, cotangent in (
        (joined, edge_pre_back),
        (edge_hid, edge_lin_back),
        (node_cat, node_pre_back),
        (node_hid, node_lin_back),
    ):
        size = left.shape[1] // segment_count
        block = lax.dynamic_slice_in_dim(left, segment_index * size, size, 1)
        parts.append(
            lax.dot_general(
                cotangent.astype(jnp.bfloat16),
                block,
                (((0,), (0,)), ((), ())),
                preferred_element_type=jnp.float32,
            )
        )
    vector_back = jnp.stack(
        [
            edge_pre_back.sum(0),
            edge_lin_back.sum(0),
            (message_back * edge_norm).sum(0),
            message_back.sum(0),
            node_pre_back.sum(0),
            node_lin_back.sum(0),
            (node_out_back * node_norm).sum(0),
            node_out_back.sum(0),
        ],
        0,
    )
    size = vector_back.shape[0] // segment_count
    parts.append(lax.dynamic_slice_in_dim(vector_back, segment_index * size, size, 0).T)
    packed = jnp.concatenate(parts, 1)
    group = lax.axis_size("dom") * lax.axis_size("dp")
    pieces = packed.reshape(group, packed.shape[0] // group, packed.shape[1])
    received = lax.all_to_all(pieces, ("dom", "dp"), 0, 0, tiled=True)
    return received.sum(0)


def own_layer_grads(reduced, sizes):
    exchanged = lax.all_to_all(jnp.stack(reduced), "segment", 0, 0, tiled=True)
    results = []
    start = 0
    for size in sizes:
        part = jnp.transpose(exchanged[:, :, start : start + size], (0, 2, 1))
        results.append(flatten_rows(part)[None])
        start += size
    return results


def local(
    node_in,
    edge_in,
    node_cot,
    edge_cot,
    send_rows,
    sender_row,
    receiver_row,
    edge_count,
    edge_w1,
    edge_w2,
    node_w1,
    node_w2,
    vectors,
):
    segment_index = lax.axis_index("segment")
    edge_total = edge_in.shape[1]
    margin = send_rows.shape[0] // 2
    live_mask = (jnp.arange(edge_total, dtype=jnp.int32) < edge_count[0]).astype(jnp.float32)
    graph_lists = (sender_row, receiver_row, live_mask)
    layers = gather_weights((edge_w1, edge_w2, node_w1, node_w2, vectors))
    edge_zero = jnp.zeros(edge_in.shape, jnp.float32)
    node_zero = jnp.zeros(node_in.shape, jnp.float32)
    probes = (edge_zero, edge_zero, edge_zero, node_zero, node_zero, node_zero)
    pick_sent = (
        send_rows[:, None] == jnp.arange(node_in.shape[1], dtype=jnp.int32)[None, :]
    ).astype(jnp.bfloat16)

    node_h = node_in
    edge_h = edge_in
    pullbacks = []
    node_outs = []
    edge_outs = []
    for weights in layers:
        halo_h = exchange(jnp.take(node_h, send_rows, axis=1), margin)
        (node_next, edge_next), pullback, saved = jax.vjp(
            batched_layer(weights, graph_lists),
            node_h.astype(jnp.float32),
            halo_h.astype(jnp.float32),
            edge_h.astype(jnp.float32),
            probes,
            has_aux=True,
        )
        pullbacks.append((pullback, saved))
        node_h = node_next.astype(jnp.bfloat16)
        edge_h = edge_next.astype(jnp.bfloat16)
        node_outs.append(node_h)
        edge_outs.append(edge_h)

    node_back = node_cot.astype(jnp.float32)
    edge_back = edge_cot.astype(jnp.float32)
    node_grads = [None] * len(layers)
    edge_grads = [None] * len(layers)
    grads = [None] * len(layers)
    for layer_index in reversed(range(len(layers))):
        pullback, saved = pullbacks[layer_index]
        node_back, halo_back, edge_back, probe_back = pullback((node_back, edge_back))
        returned = exchange(halo_back.astype(jnp.bfloat16), margin)
        node_back = node_back + jnp.einsum(
            "kn,skd->snd", pick_sent, returned, preferred_element_type=jnp.float32
        )
        node_grads[layer_index] = node_back
        edge_grads[layer_index] = edge_back
        grads[layer_index] = layer_grad_block(
            tuple(flatten_rows(value) for value in saved),
            tuple(flatten_rows(value) for value in probe_back),
        )
    segment_count = lax.axis_size("segment")
    sizes = [
        value.shape[1] // segment_count for value in (edge_w1, edge_w2, node_w1, node_w2, vectors)
    ]
    own = own_layer_grads(grads, sizes)

    def mine(values):
        return lax.dynamic_index_in_dim(jnp.stack(values), segment_index, 0, keepdims=True)

    return (
        mine(node_outs),
        mine(edge_outs),
        mine(node_grads),
        mine(edge_grads),
        own[0],
        own[1],
        own[2],
        own[3],
        own[4],
    )


def solution(mesh):
    in_specs = (
        P("dp", "dom", None),
        P("dp", "dom", None),
        P("dp", "dom", None),
        P("dp", "dom", None),
        P("dom"),
        P("dom"),
        P("dom"),
        P("dom"),
        P("segment", None, None),
        P("segment", None, None),
        P("segment", None, None),
        P("segment", None, None),
        P("segment", None, None),
    )
    out_specs = (
        P("segment", "dp", "dom", None),
        P("segment", "dp", "dom", None),
        P("segment", "dp", "dom", None),
        P("segment", "dp", "dom", None),
        P("segment", None, ("dom", "dp")),
        P("segment", None, ("dom", "dp")),
        P("segment", None, ("dom", "dp")),
        P("segment", None, ("dom", "dp")),
        P("segment", None, ("dom", "dp")),
    )
    return jax.shard_map(local, mesh=mesh, in_specs=in_specs, out_specs=out_specs, check_vma=False)
```

```python
import jax
import jax.numpy as jnp
from jax import lax
from jax.sharding import PartitionSpec as P


def layer_norm(values):
    average = jnp.mean(values, -1, keepdims=True)
    centred = values - average
    return centred * lax.rsqrt(jnp.mean(centred * centred, -1, keepdims=True) + 1e-05)


def layer_local(node_rows, halo_rows, edge_rows, probes, weights, graph_lists):
    edge_w1, edge_w2, node_w1, node_w2, vectors = weights
    sender_row, receiver_row, live_mask = graph_lists
    coeffs = vectors.astype(jnp.float32)
    node_half = node_rows.astype(jnp.bfloat16)
    node_table = jnp.concatenate([node_half, halo_rows.astype(jnp.bfloat16)], 0)
    pick_send = (
        sender_row[:, None] == jnp.arange(node_table.shape[0], dtype=jnp.int32)[None, :]
    ).astype(jnp.bfloat16)
    pick_recv = (
        receiver_row[:, None] == jnp.arange(node_rows.shape[0], dtype=jnp.int32)[None, :]
    ).astype(jnp.bfloat16)
    senders = jnp.dot(pick_send, node_table, preferred_element_type=jnp.float32).astype(
        jnp.bfloat16
    )
    receivers = jnp.dot(pick_recv, node_half, preferred_element_type=jnp.float32).astype(
        jnp.bfloat16
    )
    joined = jnp.concatenate([edge_rows.astype(jnp.bfloat16), senders, receivers], 1)
    edge_pre = jnp.dot(joined, edge_w1, preferred_element_type=jnp.float32) + coeffs[0] + probes[0]
    edge_hid = jax.nn.silu(edge_pre).astype(jnp.bfloat16)
    edge_lin = (
        jnp.dot(edge_hid, edge_w2, preferred_element_type=jnp.float32) + coeffs[1] + probes[1]
    )
    edge_norm = layer_norm(edge_lin)
    message = (edge_norm * coeffs[2] + coeffs[3] + probes[2]) * live_mask[:, None]
    edge_next = edge_rows + message
    incoming = lax.dot_general(
        pick_recv,
        message.astype(jnp.bfloat16),
        (((0,), (0,)), ((), ())),
        preferred_element_type=jnp.float32,
    )
    node_cat = jnp.concatenate([node_half, incoming.astype(jnp.bfloat16)], 1)
    node_pre = (
        jnp.dot(node_cat, node_w1, preferred_element_type=jnp.float32) + coeffs[4] + probes[3]
    )
    node_hid = jax.nn.silu(node_pre).astype(jnp.bfloat16)
    node_lin = (
        jnp.dot(node_hid, node_w2, preferred_element_type=jnp.float32) + coeffs[5] + probes[4]
    )
    node_norm = layer_norm(node_lin)
    node_next = node_rows + node_norm * coeffs[6] + coeffs[7] + probes[5]
    return ((node_next, edge_next), (joined, edge_hid, edge_norm, node_cat, node_hid, node_norm))


def batched_layer(weights, graph_lists):

    def one(node_rows, halo_rows, edge_rows, probes):
        return layer_local(node_rows, halo_rows, edge_rows, probes, weights, graph_lists)

    return jax.vmap(one)


def flatten_rows(buffer):
    return buffer.reshape(-1, buffer.shape[-1])


def exchange(rows, margin):
    count = lax.axis_size("dom")
    from_prev = lax.ppermute(rows[:, margin:], "dom", [(i, (i + 1) % count) for i in range(count)])
    from_next = lax.ppermute(rows[:, :margin], "dom", [((i + 1) % count, i) for i in range(count)])
    return jnp.concatenate([from_prev, from_next], 1)


def gather_weights(params):
    shapes = [value.shape[1:] for value in params]
    packed = jnp.concatenate([value[0] for value in params], 0)
    share_count = lax.axis_size("dp")
    total = packed.shape[0]
    padded_total = -(-total // (8 * share_count)) * (8 * share_count)
    packed = jnp.pad(packed, ((0, padded_total - total), (0, 0)))
    share = padded_total // share_count
    piece = lax.dynamic_slice_in_dim(packed, lax.axis_index("dp") * share, share, 0)
    gathered = lax.all_gather(piece, ("segment", "dp"), axis=0, tiled=False)
    layer_count = gathered.shape[0] // share_count
    gathered = gathered.reshape(layer_count, padded_total, packed.shape[1])
    layers = []
    for layer_index in range(layer_count):
        start = 0
        parts = []
        for shape in shapes:
            parts.append(gathered[layer_index, start : start + shape[0]])
            start += shape[0]
        layers.append(tuple(parts))
    return layers


def layer_grad_block(saved, probe_back):
    segment_count = lax.axis_size("segment")
    segment_index = lax.axis_index("segment")
    joined, edge_hid, edge_norm, node_cat, node_hid, node_norm = saved
    edge_pre_back, edge_lin_back, message_back, node_pre_back, node_lin_back, node_out_back = (
        probe_back
    )
    parts = []
    for left, cotangent in (
        (joined, edge_pre_back),
        (edge_hid, edge_lin_back),
        (node_cat, node_pre_back),
        (node_hid, node_lin_back),
    ):
        size = left.shape[1] // segment_count
        block = lax.dynamic_slice_in_dim(left, segment_index * size, size, 1)
        parts.append(
            lax.dot_general(
                cotangent.astype(jnp.bfloat16),
                block,
                (((0,), (0,)), ((), ())),
                preferred_element_type=jnp.float32,
            )
        )
    vector_back = jnp.stack(
        [
            edge_pre_back.sum(0),
            edge_lin_back.sum(0),
            (message_back * edge_norm).sum(0),
            message_back.sum(0),
            node_pre_back.sum(0),
            node_lin_back.sum(0),
            (node_out_back * node_norm).sum(0),
            node_out_back.sum(0),
        ],
        0,
    )
    size = vector_back.shape[0] // segment_count
    parts.append(lax.dynamic_slice_in_dim(vector_back, segment_index * size, size, 0).T)
    packed = jnp.concatenate(parts, 1)
    return lax.psum_scatter(packed, ("dom", "dp"), scatter_dimension=0, tiled=True)


def own_layer_grads(reduced, sizes):
    exchanged = lax.all_to_all(jnp.stack(reduced), "segment", 0, 0, tiled=True)
    results = []
    start = 0
    for size in sizes:
        part = jnp.transpose(exchanged[:, :, start : start + size], (0, 2, 1))
        results.append(flatten_rows(part)[None])
        start += size
    return results


def local(
    node_in,
    edge_in,
    node_cot,
    edge_cot,
    send_rows,
    sender_row,
    receiver_row,
    edge_count,
    edge_w1,
    edge_w2,
    node_w1,
    node_w2,
    vectors,
):
    segment_index = lax.axis_index("segment")
    edge_total = edge_in.shape[1]
    margin = send_rows.shape[0] // 2
    live_mask = (jnp.arange(edge_total, dtype=jnp.int32) < edge_count[0]).astype(jnp.float32)
    graph_lists = (sender_row, receiver_row, live_mask)
    layers = gather_weights((edge_w1, edge_w2, node_w1, node_w2, vectors))
    edge_zero = jnp.zeros(edge_in.shape, jnp.float32)
    node_zero = jnp.zeros(node_in.shape, jnp.float32)
    probes = (edge_zero, edge_zero, edge_zero, node_zero, node_zero, node_zero)
    pick_sent = (
        send_rows[:, None] == jnp.arange(node_in.shape[1], dtype=jnp.int32)[None, :]
    ).astype(jnp.bfloat16)

    node_h = node_in
    edge_h = edge_in
    pullbacks = []
    node_outs = []
    edge_outs = []
    for weights in layers:
        halo_h = exchange(jnp.take(node_h, send_rows, axis=1), margin)
        (node_next, edge_next), pullback, saved = jax.vjp(
            batched_layer(weights, graph_lists),
            node_h.astype(jnp.float32),
            halo_h.astype(jnp.float32),
            edge_h.astype(jnp.float32),
            probes,
            has_aux=True,
        )
        pullbacks.append((pullback, saved))
        node_h = node_next.astype(jnp.bfloat16)
        edge_h = edge_next.astype(jnp.bfloat16)
        node_outs.append(node_h)
        edge_outs.append(edge_h)

    node_back = node_cot.astype(jnp.float32)
    edge_back = edge_cot.astype(jnp.float32)
    node_grads = [None] * len(layers)
    edge_grads = [None] * len(layers)
    grads = [None] * len(layers)
    for layer_index in reversed(range(len(layers))):
        pullback, saved = pullbacks[layer_index]
        node_back, halo_back, edge_back, probe_back = pullback((node_back, edge_back))
        returned = exchange(halo_back.astype(jnp.bfloat16), margin)
        node_back = node_back + jnp.einsum(
            "kn,skd->snd", pick_sent, returned, preferred_element_type=jnp.float32
        )
        node_grads[layer_index] = node_back
        edge_grads[layer_index] = edge_back
        grads[layer_index] = layer_grad_block(
            tuple(flatten_rows(value) for value in saved),
            tuple(flatten_rows(value) for value in probe_back),
        )
    segment_count = lax.axis_size("segment")
    sizes = [
        value.shape[1] // segment_count for value in (edge_w1, edge_w2, node_w1, node_w2, vectors)
    ]
    own = own_layer_grads(grads, sizes)

    def mine(values):
        return lax.dynamic_index_in_dim(jnp.stack(values), segment_index, 0, keepdims=True)

    return (
        mine(node_outs),
        mine(edge_outs),
        mine(node_grads),
        mine(edge_grads),
        own[0],
        own[1],
        own[2],
        own[3],
        own[4],
    )


def solution(mesh):
    in_specs = (
        P("dp", "dom", None),
        P("dp", "dom", None),
        P("dp", "dom", None),
        P("dp", "dom", None),
        P("dom"),
        P("dom"),
        P("dom"),
        P("dom"),
        P("segment", None, None),
        P("segment", None, None),
        P("segment", None, None),
        P("segment", None, None),
        P("segment", None, None),
    )
    out_specs = (
        P("segment", "dp", "dom", None),
        P("segment", "dp", "dom", None),
        P("segment", "dp", "dom", None),
        P("segment", "dp", "dom", None),
        P("segment", None, ("dom", "dp")),
        P("segment", None, ("dom", "dp")),
        P("segment", None, ("dom", "dp")),
        P("segment", None, ("dom", "dp")),
        P("segment", None, ("dom", "dp")),
    )
    return jax.shard_map(local, mesh=mesh, in_specs=in_specs, out_specs=out_specs, check_vma=False)
```

```python
import jax
import jax.numpy as jnp
from jax import lax
from jax.sharding import PartitionSpec as P


def layer_norm(values):
    average = jnp.mean(values, -1, keepdims=True)
    centred = values - average
    return centred * lax.rsqrt(jnp.mean(centred * centred, -1, keepdims=True) + 1e-05)


def layer_local(node_rows, halo_rows, edge_rows, probes, weights, graph_lists):
    edge_w1, edge_w2, node_w1, node_w2, vectors = weights
    sender_row, receiver_row, live_mask = graph_lists
    coeffs = vectors.astype(jnp.float32)
    node_half = node_rows.astype(jnp.bfloat16)
    node_table = jnp.concatenate([node_half, halo_rows.astype(jnp.bfloat16)], 0)
    pick_send = (
        sender_row[:, None] == jnp.arange(node_table.shape[0], dtype=jnp.int32)[None, :]
    ).astype(jnp.bfloat16)
    pick_recv = (
        receiver_row[:, None] == jnp.arange(node_rows.shape[0], dtype=jnp.int32)[None, :]
    ).astype(jnp.bfloat16)
    senders = jnp.dot(pick_send, node_table, preferred_element_type=jnp.float32).astype(
        jnp.bfloat16
    )
    receivers = jnp.dot(pick_recv, node_half, preferred_element_type=jnp.float32).astype(
        jnp.bfloat16
    )
    joined = jnp.concatenate([edge_rows.astype(jnp.bfloat16), senders, receivers], 1)
    edge_pre = jnp.dot(joined, edge_w1, preferred_element_type=jnp.float32) + coeffs[0] + probes[0]
    edge_hid = jax.nn.silu(edge_pre).astype(jnp.bfloat16)
    edge_lin = (
        jnp.dot(edge_hid, edge_w2, preferred_element_type=jnp.float32) + coeffs[1] + probes[1]
    )
    edge_norm = layer_norm(edge_lin)
    message = (edge_norm * coeffs[2] + coeffs[3] + probes[2]) * live_mask[:, None]
    edge_next = edge_rows + message
    incoming = lax.dot_general(
        pick_recv,
        message.astype(jnp.bfloat16),
        (((0,), (0,)), ((), ())),
        preferred_element_type=jnp.float32,
    )
    node_cat = jnp.concatenate([node_half, incoming.astype(jnp.bfloat16)], 1)
    node_pre = (
        jnp.dot(node_cat, node_w1, preferred_element_type=jnp.float32) + coeffs[4] + probes[3]
    )
    node_hid = jax.nn.silu(node_pre).astype(jnp.bfloat16)
    node_lin = (
        jnp.dot(node_hid, node_w2, preferred_element_type=jnp.float32) + coeffs[5] + probes[4]
    )
    node_norm = layer_norm(node_lin)
    node_next = node_rows + node_norm * coeffs[6] + coeffs[7] + probes[5]
    return ((node_next, edge_next), (joined, edge_hid, edge_norm, node_cat, node_hid, node_norm))


def batched_layer(weights, graph_lists):

    def one(node_rows, halo_rows, edge_rows, probes):
        return layer_local(node_rows, halo_rows, edge_rows, probes, weights, graph_lists)

    return jax.vmap(one)


def flatten_rows(buffer):
    return buffer.reshape(-1, buffer.shape[-1])


def exchange(rows, margin):
    count = lax.axis_size("dom")
    from_prev = lax.ppermute(rows[:, margin:], "dom", [(i, (i + 1) % count) for i in range(count)])
    from_next = lax.ppermute(rows[:, :margin], "dom", [((i + 1) % count, i) for i in range(count)])
    return jnp.concatenate([from_prev, from_next], 1)


def gather_weights(params):
    shapes = [value.shape[1:] for value in params]
    packed = jnp.concatenate([value[0] for value in params], 0)
    share_count = lax.axis_size("dp")
    total = packed.shape[0]
    padded_total = -(-total // (8 * share_count)) * (8 * share_count)
    packed = jnp.pad(packed, ((0, padded_total - total), (0, 0)))
    share = padded_total // share_count
    piece = lax.dynamic_slice_in_dim(packed, lax.axis_index("dp") * share, share, 0)
    gathered = lax.all_gather(piece, ("segment", "dp"), axis=0, tiled=False)
    layer_count = gathered.shape[0] // share_count
    gathered = gathered.reshape(layer_count, padded_total, packed.shape[1])
    layers = []
    for layer_index in range(layer_count):
        start = 0
        parts = []
        for shape in shapes:
            parts.append(gathered[layer_index, start : start + shape[0]])
            start += shape[0]
        layers.append(tuple(parts))
    return layers


def layer_grad_block(saved, probe_back):
    segment_count = lax.axis_size("segment")
    segment_index = lax.axis_index("segment")
    joined, edge_hid, edge_norm, node_cat, node_hid, node_norm = saved
    edge_pre_back, edge_lin_back, message_back, node_pre_back, node_lin_back, node_out_back = (
        probe_back
    )
    parts = []
    for left, cotangent in (
        (joined, edge_pre_back),
        (edge_hid, edge_lin_back),
        (node_cat, node_pre_back),
        (node_hid, node_lin_back),
    ):
        size = left.shape[1] // segment_count
        block = lax.dynamic_slice_in_dim(left, segment_index * size, size, 1)
        parts.append(
            lax.dot_general(
                cotangent.astype(jnp.bfloat16),
                block,
                (((0,), (0,)), ((), ())),
                preferred_element_type=jnp.float32,
            )
        )
    vector_back = jnp.stack(
        [
            edge_pre_back.sum(0),
            edge_lin_back.sum(0),
            (message_back * edge_norm).sum(0),
            message_back.sum(0),
            node_pre_back.sum(0),
            node_lin_back.sum(0),
            (node_out_back * node_norm).sum(0),
            node_out_back.sum(0),
        ],
        0,
    )
    size = vector_back.shape[0] // segment_count
    parts.append(lax.dynamic_slice_in_dim(vector_back, segment_index * size, size, 0).T)
    packed = jnp.concatenate(parts, 1)
    dom_count = lax.axis_size("dom")
    dp_count = lax.axis_size("dp")
    dp_index = lax.axis_index("dp")
    blocks = packed.reshape(dom_count, dp_count, packed.shape[0] // (dom_count * dp_count), -1)
    kept = lax.dynamic_index_in_dim(blocks, dp_index, 1, keepdims=False)
    sent = lax.dynamic_index_in_dim(blocks, dp_count - 1 - dp_index, 1, keepdims=False)
    summed = kept + lax.ppermute(sent, "dp", [(i, dp_count - 1 - i) for i in range(dp_count)])
    received = lax.all_to_all(summed, "dom", 0, 0, tiled=True)
    return received.sum(0)


def own_layer_grads(reduced, sizes):
    exchanged = lax.all_to_all(jnp.stack(reduced), "segment", 0, 0, tiled=True)
    results = []
    start = 0
    for size in sizes:
        part = jnp.transpose(exchanged[:, :, start : start + size], (0, 2, 1))
        results.append(flatten_rows(part)[None])
        start += size
    return results


def local(
    node_in,
    edge_in,
    node_cot,
    edge_cot,
    send_rows,
    sender_row,
    receiver_row,
    edge_count,
    edge_w1,
    edge_w2,
    node_w1,
    node_w2,
    vectors,
):
    segment_index = lax.axis_index("segment")
    edge_total = edge_in.shape[1]
    margin = send_rows.shape[0] // 2
    live_mask = (jnp.arange(edge_total, dtype=jnp.int32) < edge_count[0]).astype(jnp.float32)
    graph_lists = (sender_row, receiver_row, live_mask)
    layers = gather_weights((edge_w1, edge_w2, node_w1, node_w2, vectors))
    edge_zero = jnp.zeros(edge_in.shape, jnp.float32)
    node_zero = jnp.zeros(node_in.shape, jnp.float32)
    probes = (edge_zero, edge_zero, edge_zero, node_zero, node_zero, node_zero)
    pick_sent = (
        send_rows[:, None] == jnp.arange(node_in.shape[1], dtype=jnp.int32)[None, :]
    ).astype(jnp.bfloat16)

    node_h = node_in
    edge_h = edge_in
    pullbacks = []
    node_outs = []
    edge_outs = []
    for weights in layers:
        halo_h = exchange(jnp.take(node_h, send_rows, axis=1), margin)
        (node_next, edge_next), pullback, saved = jax.vjp(
            batched_layer(weights, graph_lists),
            node_h.astype(jnp.float32),
            halo_h.astype(jnp.float32),
            edge_h.astype(jnp.float32),
            probes,
            has_aux=True,
        )
        pullbacks.append((pullback, saved))
        node_h = node_next.astype(jnp.bfloat16)
        edge_h = edge_next.astype(jnp.bfloat16)
        node_outs.append(node_h)
        edge_outs.append(edge_h)

    node_back = node_cot.astype(jnp.float32)
    edge_back = edge_cot.astype(jnp.float32)
    node_grads = [None] * len(layers)
    edge_grads = [None] * len(layers)
    grads = [None] * len(layers)
    for layer_index in reversed(range(len(layers))):
        pullback, saved = pullbacks[layer_index]
        node_back, halo_back, edge_back, probe_back = pullback((node_back, edge_back))
        returned = exchange(halo_back.astype(jnp.bfloat16), margin)
        node_back = node_back + jnp.einsum(
            "kn,skd->snd", pick_sent, returned, preferred_element_type=jnp.float32
        )
        node_grads[layer_index] = node_back
        edge_grads[layer_index] = edge_back
        grads[layer_index] = layer_grad_block(
            tuple(flatten_rows(value) for value in saved),
            tuple(flatten_rows(value) for value in probe_back),
        )
    segment_count = lax.axis_size("segment")
    sizes = [
        value.shape[1] // segment_count for value in (edge_w1, edge_w2, node_w1, node_w2, vectors)
    ]
    own = own_layer_grads(grads, sizes)

    def mine(values):
        return lax.dynamic_index_in_dim(jnp.stack(values), segment_index, 0, keepdims=True)

    return (
        mine(node_outs),
        mine(edge_outs),
        mine(node_grads),
        mine(edge_grads),
        own[0],
        own[1],
        own[2],
        own[3],
        own[4],
    )


def solution(mesh):
    in_specs = (
        P("dp", "dom", None),
        P("dp", "dom", None),
        P("dp", "dom", None),
        P("dp", "dom", None),
        P("dom"),
        P("dom"),
        P("dom"),
        P("dom"),
        P("segment", None, None),
        P("segment", None, None),
        P("segment", None, None),
        P("segment", None, None),
        P("segment", None, None),
    )
    out_specs = (
        P("segment", "dp", "dom", None),
        P("segment", "dp", "dom", None),
        P("segment", "dp", "dom", None),
        P("segment", "dp", "dom", None),
        P("segment", None, ("dom", "dp")),
        P("segment", None, ("dom", "dp")),
        P("segment", None, ("dom", "dp")),
        P("segment", None, ("dom", "dp")),
        P("segment", None, ("dom", "dp")),
    )
    return jax.shard_map(local, mesh=mesh, in_specs=in_specs, out_specs=out_specs, check_vma=False)
```

```python
import jax
import jax.numpy as jnp
from jax import lax
from jax.sharding import PartitionSpec as P


def layer_norm(values):
    average = jnp.mean(values, -1, keepdims=True)
    centred = values - average
    return centred * lax.rsqrt(jnp.mean(centred * centred, -1, keepdims=True) + 1e-05)


def layer_local(node_rows, halo_rows, edge_rows, probes, weights, graph_lists):
    edge_w1, edge_w2, node_w1, node_w2, vectors = weights
    sender_row, receiver_row, live_mask = graph_lists
    coeffs = vectors.astype(jnp.float32)
    node_half = node_rows.astype(jnp.bfloat16)
    node_table = jnp.concatenate([node_half, halo_rows.astype(jnp.bfloat16)], 0)
    pick_send = (
        sender_row[:, None] == jnp.arange(node_table.shape[0], dtype=jnp.int32)[None, :]
    ).astype(jnp.bfloat16)
    pick_recv = (
        receiver_row[:, None] == jnp.arange(node_rows.shape[0], dtype=jnp.int32)[None, :]
    ).astype(jnp.bfloat16)
    senders = jnp.dot(pick_send, node_table, preferred_element_type=jnp.float32).astype(
        jnp.bfloat16
    )
    receivers = jnp.dot(pick_recv, node_half, preferred_element_type=jnp.float32).astype(
        jnp.bfloat16
    )
    joined = jnp.concatenate([edge_rows.astype(jnp.bfloat16), senders, receivers], 1)
    edge_pre = jnp.dot(joined, edge_w1, preferred_element_type=jnp.float32) + coeffs[0] + probes[0]
    edge_hid = jax.nn.silu(edge_pre).astype(jnp.bfloat16)
    edge_lin = (
        jnp.dot(edge_hid, edge_w2, preferred_element_type=jnp.float32) + coeffs[1] + probes[1]
    )
    edge_norm = layer_norm(edge_lin)
    message = (edge_norm * coeffs[2] + coeffs[3] + probes[2]) * live_mask[:, None]
    edge_next = edge_rows + message
    incoming = lax.dot_general(
        pick_recv,
        message.astype(jnp.bfloat16),
        (((0,), (0,)), ((), ())),
        preferred_element_type=jnp.float32,
    )
    node_cat = jnp.concatenate([node_half, incoming.astype(jnp.bfloat16)], 1)
    node_pre = (
        jnp.dot(node_cat, node_w1, preferred_element_type=jnp.float32) + coeffs[4] + probes[3]
    )
    node_hid = jax.nn.silu(node_pre).astype(jnp.bfloat16)
    node_lin = (
        jnp.dot(node_hid, node_w2, preferred_element_type=jnp.float32) + coeffs[5] + probes[4]
    )
    node_norm = layer_norm(node_lin)
    node_next = node_rows + node_norm * coeffs[6] + coeffs[7] + probes[5]
    return ((node_next, edge_next), (joined, edge_hid, edge_norm, node_cat, node_hid, node_norm))


def batched_layer(weights, graph_lists):

    def one(node_rows, halo_rows, edge_rows, probes):
        return layer_local(node_rows, halo_rows, edge_rows, probes, weights, graph_lists)

    return jax.vmap(one)


def flatten_rows(buffer):
    return buffer.reshape(-1, buffer.shape[-1])


def exchange(rows, margin):
    count = lax.axis_size("dom")
    from_prev = lax.ppermute(rows[:, margin:], "dom", [(i, (i + 1) % count) for i in range(count)])
    from_next = lax.ppermute(rows[:, :margin], "dom", [((i + 1) % count, i) for i in range(count)])
    return jnp.concatenate([from_prev, from_next], 1)


def gather_weights(params):
    shapes = [value.shape[1:] for value in params]
    packed = jnp.concatenate([value[0] for value in params], 0)
    share_count = lax.axis_size("dp")
    total = packed.shape[0]
    padded_total = -(-total // (8 * share_count)) * (8 * share_count)
    packed = jnp.pad(packed, ((0, padded_total - total), (0, 0)))
    share = padded_total // share_count
    piece = lax.dynamic_slice_in_dim(packed, lax.axis_index("dp") * share, share, 0)
    gathered = lax.all_gather(piece, ("segment", "dp"), axis=0, tiled=False)
    layer_count = gathered.shape[0] // share_count
    gathered = gathered.reshape(layer_count, padded_total, packed.shape[1])
    layers = []
    for layer_index in range(layer_count):
        start = 0
        parts = []
        for shape in shapes:
            parts.append(gathered[layer_index, start : start + shape[0]])
            start += shape[0]
        layers.append(tuple(parts))
    return layers


def layer_grad_block(saved, probe_back):
    segment_count = lax.axis_size("segment")
    segment_index = lax.axis_index("segment")
    joined, edge_hid, edge_norm, node_cat, node_hid, node_norm = saved
    edge_pre_back, edge_lin_back, message_back, node_pre_back, node_lin_back, node_out_back = (
        probe_back
    )
    parts = []
    for left, cotangent in (
        (joined, edge_pre_back),
        (edge_hid, edge_lin_back),
        (node_cat, node_pre_back),
        (node_hid, node_lin_back),
    ):
        size = left.shape[1] // segment_count
        block = lax.dynamic_slice_in_dim(left, segment_index * size, size, 1)
        parts.append(
            lax.dot_general(
                block,
                cotangent.astype(jnp.bfloat16),
                (((0,), (0,)), ((), ())),
                preferred_element_type=jnp.float32,
            )
        )
    vector_back = jnp.stack(
        [
            edge_pre_back.sum(0),
            edge_lin_back.sum(0),
            (message_back * edge_norm).sum(0),
            message_back.sum(0),
            node_pre_back.sum(0),
            node_lin_back.sum(0),
            (node_out_back * node_norm).sum(0),
            node_out_back.sum(0),
        ],
        0,
    )
    size = vector_back.shape[0] // segment_count
    parts.append(lax.dynamic_slice_in_dim(vector_back, segment_index * size, size, 0))
    height = sum(part.shape[0] for part in parts)
    parts.append(jnp.zeros((-height % 8, vector_back.shape[1]), jnp.float32))
    return jnp.concatenate(parts, 0)


def reduce_grads(packed):
    return lax.psum_scatter(packed, ("dom", "dp"), scatter_dimension=1, tiled=True)


def own_layer_grads(reduced, sizes):
    exchanged = lax.all_to_all(jnp.stack(reduced), "segment", 0, 0, tiled=True)
    results = []
    start = 0
    for size in sizes:
        results.append(flatten_rows(exchanged[:, start : start + size])[None])
        start += size
    return results


def local(
    node_in,
    edge_in,
    node_cot,
    edge_cot,
    send_rows,
    sender_row,
    receiver_row,
    edge_count,
    edge_w1,
    edge_w2,
    node_w1,
    node_w2,
    vectors,
):
    segment_index = lax.axis_index("segment")
    edge_total = edge_in.shape[1]
    margin = send_rows.shape[0] // 2
    live_mask = (jnp.arange(edge_total, dtype=jnp.int32) < edge_count[0]).astype(jnp.float32)
    graph_lists = (sender_row, receiver_row, live_mask)
    layers = gather_weights((edge_w1, edge_w2, node_w1, node_w2, vectors))
    edge_zero = jnp.zeros(edge_in.shape, jnp.float32)
    node_zero = jnp.zeros(node_in.shape, jnp.float32)
    probes = (edge_zero, edge_zero, edge_zero, node_zero, node_zero, node_zero)
    pick_sent = (
        send_rows[:, None] == jnp.arange(node_in.shape[1], dtype=jnp.int32)[None, :]
    ).astype(jnp.bfloat16)

    node_h = node_in
    edge_h = edge_in
    pullbacks = []
    node_outs = []
    edge_outs = []
    for weights in layers:
        halo_h = exchange(jnp.take(node_h, send_rows, axis=1), margin)
        (node_next, edge_next), pullback, saved = jax.vjp(
            batched_layer(weights, graph_lists),
            node_h.astype(jnp.float32),
            halo_h.astype(jnp.float32),
            edge_h.astype(jnp.float32),
            probes,
            has_aux=True,
        )
        pullbacks.append((pullback, saved))
        node_h = node_next.astype(jnp.bfloat16)
        edge_h = edge_next.astype(jnp.bfloat16)
        node_outs.append(node_h)
        edge_outs.append(edge_h)

    node_back = node_cot.astype(jnp.float32)
    edge_back = edge_cot.astype(jnp.float32)
    node_grads = [None] * len(layers)
    edge_grads = [None] * len(layers)
    grads = [None] * len(layers)
    for layer_index in reversed(range(len(layers))):
        pullback, saved = pullbacks[layer_index]
        node_back, halo_back, edge_back, probe_back = pullback((node_back, edge_back))
        returned = exchange(halo_back.astype(jnp.bfloat16), margin)
        node_back = node_back + jnp.einsum(
            "kn,skd->snd", pick_sent, returned, preferred_element_type=jnp.float32
        )
        node_grads[layer_index] = node_back
        edge_grads[layer_index] = edge_back
        grads[layer_index] = layer_grad_block(
            tuple(flatten_rows(value) for value in saved),
            tuple(flatten_rows(value) for value in probe_back),
        )
        if layer_index % 2 == 0:
            pair = jnp.concatenate(grads[layer_index : layer_index + 2], 0)
            if layer_index == 0:
                pair, node_grads[0] = lax.optimization_barrier((pair, node_grads[0]))
            reduced = reduce_grads(pair)
            height = grads[layer_index].shape[0]
            grads[layer_index] = reduced[:height]
            if layer_index + 1 < len(layers):
                grads[layer_index + 1] = reduced[height:]
    segment_count = lax.axis_size("segment")
    sizes = [
        value.shape[1] // segment_count for value in (edge_w1, edge_w2, node_w1, node_w2, vectors)
    ]
    own = own_layer_grads(grads, sizes)

    def mine(values):
        return lax.dynamic_index_in_dim(jnp.stack(values), segment_index, 0, keepdims=True)

    return (
        mine(node_outs),
        mine(edge_outs),
        mine(node_grads),
        mine(edge_grads),
        own[0],
        own[1],
        own[2],
        own[3],
        own[4],
    )


def solution(mesh):
    in_specs = (
        P("dp", "dom", None),
        P("dp", "dom", None),
        P("dp", "dom", None),
        P("dp", "dom", None),
        P("dom"),
        P("dom"),
        P("dom"),
        P("dom"),
        P("segment", None, None),
        P("segment", None, None),
        P("segment", None, None),
        P("segment", None, None),
        P("segment", None, None),
    )
    out_specs = (
        P("segment", "dp", "dom", None),
        P("segment", "dp", "dom", None),
        P("segment", "dp", "dom", None),
        P("segment", "dp", "dom", None),
        P("segment", None, ("dom", "dp")),
        P("segment", None, ("dom", "dp")),
        P("segment", None, ("dom", "dp")),
        P("segment", None, ("dom", "dp")),
        P("segment", None, ("dom", "dp")),
    )
    return jax.shard_map(local, mesh=mesh, in_specs=in_specs, out_specs=out_specs, check_vma=False)
```

```python
import jax
import jax.numpy as jnp
from jax import lax
from jax.sharding import PartitionSpec as P


def layer_norm(values):
    average = jnp.mean(values, -1, keepdims=True)
    centred = values - average
    return centred * lax.rsqrt(jnp.mean(centred * centred, -1, keepdims=True) + 1e-05)


def layer_local(node_rows, halo_rows, edge_rows, probes, weights, graph_lists):
    edge_w1, edge_w2, node_w1, node_w2, vectors = weights
    sender_row, receiver_row, live_mask = graph_lists
    coeffs = vectors.astype(jnp.float32)
    node_half = node_rows.astype(jnp.bfloat16)
    node_table = jnp.concatenate([node_half, halo_rows.astype(jnp.bfloat16)], 0)
    pick_send = (
        sender_row[:, None] == jnp.arange(node_table.shape[0], dtype=jnp.int32)[None, :]
    ).astype(jnp.bfloat16)
    pick_recv = (
        receiver_row[:, None] == jnp.arange(node_rows.shape[0], dtype=jnp.int32)[None, :]
    ).astype(jnp.bfloat16)
    senders = jnp.dot(pick_send, node_table, preferred_element_type=jnp.float32).astype(
        jnp.bfloat16
    )
    receivers = jnp.dot(pick_recv, node_half, preferred_element_type=jnp.float32).astype(
        jnp.bfloat16
    )
    joined = jnp.concatenate([edge_rows.astype(jnp.bfloat16), senders, receivers], 1)
    edge_pre = jnp.dot(joined, edge_w1, preferred_element_type=jnp.float32) + coeffs[0] + probes[0]
    edge_hid = jax.nn.silu(edge_pre).astype(jnp.bfloat16)
    edge_lin = (
        jnp.dot(edge_hid, edge_w2, preferred_element_type=jnp.float32) + coeffs[1] + probes[1]
    )
    edge_norm = layer_norm(edge_lin)
    message = (edge_norm * coeffs[2] + coeffs[3] + probes[2]) * live_mask[:, None]
    edge_next = edge_rows + message
    incoming = lax.dot_general(
        pick_recv,
        message.astype(jnp.bfloat16),
        (((0,), (0,)), ((), ())),
        preferred_element_type=jnp.float32,
    )
    node_cat = jnp.concatenate([node_half, incoming.astype(jnp.bfloat16)], 1)
    node_pre = (
        jnp.dot(node_cat, node_w1, preferred_element_type=jnp.float32) + coeffs[4] + probes[3]
    )
    node_hid = jax.nn.silu(node_pre).astype(jnp.bfloat16)
    node_lin = (
        jnp.dot(node_hid, node_w2, preferred_element_type=jnp.float32) + coeffs[5] + probes[4]
    )
    node_norm = layer_norm(node_lin)
    node_next = node_rows + node_norm * coeffs[6] + coeffs[7] + probes[5]
    return ((node_next, edge_next), (joined, edge_hid, edge_norm, node_cat, node_hid, node_norm))


def batched_layer(weights, graph_lists):

    def one(node_rows, halo_rows, edge_rows, probes):
        return layer_local(node_rows, halo_rows, edge_rows, probes, weights, graph_lists)

    return jax.vmap(one)


def flatten_rows(buffer):
    return buffer.reshape(-1, buffer.shape[-1])


def exchange(rows, margin):
    count = lax.axis_size("dom")
    from_prev = lax.ppermute(rows[:, margin:], "dom", [(i, (i + 1) % count) for i in range(count)])
    from_next = lax.ppermute(rows[:, :margin], "dom", [((i + 1) % count, i) for i in range(count)])
    return jnp.concatenate([from_prev, from_next], 1)


def gather_weights(params):
    shapes = [value.shape[1:] for value in params]
    packed = jnp.concatenate([value[0] for value in params], 0)
    share_count = lax.axis_size("dp")
    total = packed.shape[0]
    padded_total = -(-total // (8 * share_count)) * (8 * share_count)
    packed = jnp.pad(packed, ((0, padded_total - total), (0, 0)))
    share = padded_total // share_count
    piece = lax.dynamic_slice_in_dim(packed, lax.axis_index("dp") * share, share, 0)
    gathered = lax.all_gather(piece, ("segment", "dp"), axis=0, tiled=False)
    layer_count = gathered.shape[0] // share_count
    gathered = gathered.reshape(layer_count, padded_total, packed.shape[1])
    layers = []
    for layer_index in range(layer_count):
        start = 0
        parts = []
        for shape in shapes:
            parts.append(gathered[layer_index, start : start + shape[0]])
            start += shape[0]
        layers.append(tuple(parts))
    return layers


def layer_grad_block(saved, probe_back):
    segment_count = lax.axis_size("segment")
    segment_index = lax.axis_index("segment")
    joined, edge_hid, edge_norm, node_cat, node_hid, node_norm = saved
    edge_pre_back, edge_lin_back, message_back, node_pre_back, node_lin_back, node_out_back = (
        probe_back
    )
    parts = []
    for left, cotangent in (
        (joined, edge_pre_back),
        (edge_hid, edge_lin_back),
        (node_cat, node_pre_back),
        (node_hid, node_lin_back),
    ):
        size = left.shape[1] // segment_count
        block = lax.dynamic_slice_in_dim(left, segment_index * size, size, 1)
        parts.append(
            lax.dot_general(
                cotangent.astype(jnp.bfloat16),
                block,
                (((0,), (0,)), ((), ())),
                preferred_element_type=jnp.float32,
            )
        )
    vector_back = jnp.stack(
        [
            edge_pre_back.sum(0),
            edge_lin_back.sum(0),
            (message_back * edge_norm).sum(0),
            message_back.sum(0),
            node_pre_back.sum(0),
            node_lin_back.sum(0),
            (node_out_back * node_norm).sum(0),
            node_out_back.sum(0),
        ],
        0,
    )
    size = vector_back.shape[0] // segment_count
    parts.append(lax.dynamic_slice_in_dim(vector_back, segment_index * size, size, 0).T)
    return jnp.concatenate(parts, 1)


def reduce_grads(packed):
    return lax.psum_scatter(packed, ("dom", "dp"), scatter_dimension=0, tiled=True)


def own_layer_grads(reduced, sizes):
    exchanged = lax.all_to_all(jnp.stack(reduced), "segment", 0, 0, tiled=True)
    results = []
    start = 0
    for size in sizes:
        part = jnp.transpose(exchanged[:, :, start : start + size], (0, 2, 1))
        results.append(flatten_rows(part)[None])
        start += size
    return results


def local(
    node_in,
    edge_in,
    node_cot,
    edge_cot,
    send_rows,
    sender_row,
    receiver_row,
    edge_count,
    edge_w1,
    edge_w2,
    node_w1,
    node_w2,
    vectors,
):
    segment_index = lax.axis_index("segment")
    edge_total = edge_in.shape[1]
    margin = send_rows.shape[0] // 2
    live_mask = (jnp.arange(edge_total, dtype=jnp.int32) < edge_count[0]).astype(jnp.float32)
    graph_lists = (sender_row, receiver_row, live_mask)
    layers = gather_weights((edge_w1, edge_w2, node_w1, node_w2, vectors))
    edge_zero = jnp.zeros(edge_in.shape, jnp.float32)
    node_zero = jnp.zeros(node_in.shape, jnp.float32)
    probes = (edge_zero, edge_zero, edge_zero, node_zero, node_zero, node_zero)
    pick_sent = (
        send_rows[:, None] == jnp.arange(node_in.shape[1], dtype=jnp.int32)[None, :]
    ).astype(jnp.bfloat16)

    node_h = node_in
    edge_h = edge_in
    pullbacks = []
    node_outs = []
    edge_outs = []
    for weights in layers:
        halo_h = exchange(jnp.take(node_h, send_rows, axis=1), margin)
        (node_next, edge_next), pullback, saved = jax.vjp(
            batched_layer(weights, graph_lists),
            node_h.astype(jnp.float32),
            halo_h.astype(jnp.float32),
            edge_h.astype(jnp.float32),
            probes,
            has_aux=True,
        )
        pullbacks.append((pullback, saved))
        node_h = node_next.astype(jnp.bfloat16)
        edge_h = edge_next.astype(jnp.bfloat16)
        node_outs.append(node_h)
        edge_outs.append(edge_h)

    node_back = node_cot.astype(jnp.float32)
    edge_back = edge_cot.astype(jnp.float32)
    node_grads = [None] * len(layers)
    edge_grads = [None] * len(layers)
    grads = [None] * len(layers)
    for layer_index in reversed(range(len(layers))):
        pullback, saved = pullbacks[layer_index]
        node_back, halo_back, edge_back, probe_back = pullback((node_back, edge_back))
        returned = exchange(halo_back.astype(jnp.bfloat16), margin)
        node_back = node_back + jnp.einsum(
            "kn,skd->snd", pick_sent, returned, preferred_element_type=jnp.float32
        )
        node_grads[layer_index] = node_back
        edge_grads[layer_index] = edge_back
        packed = layer_grad_block(
            tuple(flatten_rows(value) for value in saved),
            tuple(flatten_rows(value) for value in probe_back),
        )
        if layer_index == 0:
            packed, node_grads[0] = lax.optimization_barrier((packed, node_grads[0]))
        grads[layer_index] = reduce_grads(packed)
    segment_count = lax.axis_size("segment")
    sizes = [
        value.shape[1] // segment_count for value in (edge_w1, edge_w2, node_w1, node_w2, vectors)
    ]
    own = own_layer_grads(grads, sizes)

    def mine(values):
        return lax.dynamic_index_in_dim(jnp.stack(values), segment_index, 0, keepdims=True)

    return (
        mine(node_outs),
        mine(edge_outs),
        mine(node_grads),
        mine(edge_grads),
        own[0],
        own[1],
        own[2],
        own[3],
        own[4],
    )


def solution(mesh):
    in_specs = (
        P("dp", "dom", None),
        P("dp", "dom", None),
        P("dp", "dom", None),
        P("dp", "dom", None),
        P("dom"),
        P("dom"),
        P("dom"),
        P("dom"),
        P("segment", None, None),
        P("segment", None, None),
        P("segment", None, None),
        P("segment", None, None),
        P("segment", None, None),
    )
    out_specs = (
        P("segment", "dp", "dom", None),
        P("segment", "dp", "dom", None),
        P("segment", "dp", "dom", None),
        P("segment", "dp", "dom", None),
        P("segment", None, ("dom", "dp")),
        P("segment", None, ("dom", "dp")),
        P("segment", None, ("dom", "dp")),
        P("segment", None, ("dom", "dp")),
        P("segment", None, ("dom", "dp")),
    )
    return jax.shard_map(local, mesh=mesh, in_specs=in_specs, out_specs=out_specs, check_vma=False)
```

```python
import jax
import jax.numpy as jnp
from jax import lax
from jax.sharding import PartitionSpec as P


def layer_norm(values):
    average = jnp.mean(values, -1, keepdims=True)
    centred = values - average
    return centred * lax.rsqrt(jnp.mean(centred * centred, -1, keepdims=True) + 1e-05)


def layer_local(node_rows, halo_rows, edge_rows, probes, weights, graph_lists):
    edge_w1, edge_w2, node_w1, node_w2, vectors = weights
    sender_row, receiver_row, live_mask = graph_lists
    coeffs = vectors.astype(jnp.float32)
    node_half = node_rows.astype(jnp.bfloat16)
    node_table = jnp.concatenate([node_half, halo_rows.astype(jnp.bfloat16)], 0)
    pick_send = (
        sender_row[:, None] == jnp.arange(node_table.shape[0], dtype=jnp.int32)[None, :]
    ).astype(jnp.bfloat16)
    pick_recv = (
        receiver_row[:, None] == jnp.arange(node_rows.shape[0], dtype=jnp.int32)[None, :]
    ).astype(jnp.bfloat16)
    senders = jnp.dot(pick_send, node_table, preferred_element_type=jnp.float32).astype(
        jnp.bfloat16
    )
    receivers = jnp.dot(pick_recv, node_half, preferred_element_type=jnp.float32).astype(
        jnp.bfloat16
    )
    joined = jnp.concatenate([edge_rows.astype(jnp.bfloat16), senders, receivers], 1)
    edge_pre = jnp.dot(joined, edge_w1, preferred_element_type=jnp.float32) + coeffs[0] + probes[0]
    edge_hid = jax.nn.silu(edge_pre).astype(jnp.bfloat16)
    edge_lin = (
        jnp.dot(edge_hid, edge_w2, preferred_element_type=jnp.float32) + coeffs[1] + probes[1]
    )
    edge_norm = layer_norm(edge_lin)
    message = (edge_norm * coeffs[2] + coeffs[3] + probes[2]) * live_mask[:, None]
    edge_next = edge_rows + message
    incoming = lax.dot_general(
        pick_recv,
        message.astype(jnp.bfloat16),
        (((0,), (0,)), ((), ())),
        preferred_element_type=jnp.float32,
    )
    node_cat = jnp.concatenate([node_half, incoming.astype(jnp.bfloat16)], 1)
    node_pre = (
        jnp.dot(node_cat, node_w1, preferred_element_type=jnp.float32) + coeffs[4] + probes[3]
    )
    node_hid = jax.nn.silu(node_pre).astype(jnp.bfloat16)
    node_lin = (
        jnp.dot(node_hid, node_w2, preferred_element_type=jnp.float32) + coeffs[5] + probes[4]
    )
    node_norm = layer_norm(node_lin)
    node_next = node_rows + node_norm * coeffs[6] + coeffs[7] + probes[5]
    return ((node_next, edge_next), (joined, edge_hid, edge_norm, node_cat, node_hid, node_norm))


def batched_layer(weights, graph_lists):

    def one(node_rows, halo_rows, edge_rows, probes):
        return layer_local(node_rows, halo_rows, edge_rows, probes, weights, graph_lists)

    return jax.vmap(one)


def flatten_rows(buffer):
    return buffer.reshape(-1, buffer.shape[-1])


def exchange(rows, margin):
    count = lax.axis_size("dom")
    from_prev = lax.ppermute(rows[:, margin:], "dom", [(i, (i + 1) % count) for i in range(count)])
    from_next = lax.ppermute(rows[:, :margin], "dom", [((i + 1) % count, i) for i in range(count)])
    return jnp.concatenate([from_prev, from_next], 1)


def gather_weights(params):
    shapes = [value.shape[1:] for value in params]
    packed = jnp.concatenate([value[0] for value in params], 0)
    share_count = lax.axis_size("dp")
    total = packed.shape[0]
    padded_total = -(-total // (8 * share_count)) * (8 * share_count)
    packed = jnp.pad(packed, ((0, padded_total - total), (0, 0)))
    share = padded_total // share_count
    piece = lax.dynamic_slice_in_dim(packed, lax.axis_index("dp") * share, share, 0)
    gathered = lax.all_gather(piece, ("segment", "dp"), axis=0, tiled=False)
    layer_count = gathered.shape[0] // share_count
    gathered = gathered.reshape(layer_count, padded_total, packed.shape[1])
    layers = []
    for layer_index in range(layer_count):
        start = 0
        parts = []
        for shape in shapes:
            parts.append(gathered[layer_index, start : start + shape[0]])
            start += shape[0]
        layers.append(tuple(parts))
    return layers


def pair_grad_block(saved_pair, back_pair):
    segment_count = lax.axis_size("segment")
    segment_index = lax.axis_index("segment")
    parts = []
    for left_at, back_at in ((0, 0), (1, 1), (3, 3), (4, 4)):
        size = saved_pair[0][left_at].shape[1] // segment_count
        block = jnp.stack(
            [
                lax.dynamic_slice_in_dim(saved[left_at], segment_index * size, size, 1)
                for saved in saved_pair
            ]
        )
        cotangent = jnp.stack([back[back_at].astype(jnp.bfloat16) for back in back_pair])
        parts.append(
            lax.dot_general(
                cotangent,
                block,
                (((1,), (1,)), ((0,), (0,))),
                preferred_element_type=jnp.float32,
            )
        )
    vectors = []
    for saved, back in zip(saved_pair, back_pair):
        edge_norm, node_norm = saved[2], saved[5]
        edge_pre_back, edge_lin_back, message_back, node_pre_back, node_lin_back, node_out_back = (
            back
        )
        vector_back = jnp.stack(
            [
                edge_pre_back.sum(0),
                edge_lin_back.sum(0),
                (message_back * edge_norm).sum(0),
                message_back.sum(0),
                node_pre_back.sum(0),
                node_lin_back.sum(0),
                (node_out_back * node_norm).sum(0),
                node_out_back.sum(0),
            ],
            0,
        )
        size = vector_back.shape[0] // segment_count
        vectors.append(lax.dynamic_slice_in_dim(vector_back, segment_index * size, size, 0).T)
    parts.append(jnp.stack(vectors))
    packed = jnp.transpose(jnp.concatenate(parts, 2), (1, 0, 2))
    width = packed.shape[2]
    packed = packed.reshape(packed.shape[0], -1)
    reduced = lax.psum_scatter(packed, ("dom", "dp"), scatter_dimension=0, tiled=True)
    return reduced[:, :width], reduced[:, width:]


def own_layer_grads(reduced, sizes):
    exchanged = lax.all_to_all(jnp.stack(reduced), "segment", 0, 0, tiled=True)
    results = []
    start = 0
    for size in sizes:
        part = jnp.transpose(exchanged[:, :, start : start + size], (0, 2, 1))
        results.append(flatten_rows(part)[None])
        start += size
    return results


def local(
    node_in,
    edge_in,
    node_cot,
    edge_cot,
    send_rows,
    sender_row,
    receiver_row,
    edge_count,
    edge_w1,
    edge_w2,
    node_w1,
    node_w2,
    vectors,
):
    segment_index = lax.axis_index("segment")
    edge_total = edge_in.shape[1]
    margin = send_rows.shape[0] // 2
    live_mask = (jnp.arange(edge_total, dtype=jnp.int32) < edge_count[0]).astype(jnp.float32)
    graph_lists = (sender_row, receiver_row, live_mask)
    layers = gather_weights((edge_w1, edge_w2, node_w1, node_w2, vectors))
    edge_zero = jnp.zeros(edge_in.shape, jnp.float32)
    node_zero = jnp.zeros(node_in.shape, jnp.float32)
    probes = (edge_zero, edge_zero, edge_zero, node_zero, node_zero, node_zero)
    pick_sent = (
        send_rows[:, None] == jnp.arange(node_in.shape[1], dtype=jnp.int32)[None, :]
    ).astype(jnp.bfloat16)

    node_h = node_in
    edge_h = edge_in
    pullbacks = []
    node_outs = []
    edge_outs = []
    for weights in layers:
        halo_h = exchange(jnp.take(node_h, send_rows, axis=1), margin)
        (node_next, edge_next), pullback, saved = jax.vjp(
            batched_layer(weights, graph_lists),
            node_h.astype(jnp.float32),
            halo_h.astype(jnp.float32),
            edge_h.astype(jnp.float32),
            probes,
            has_aux=True,
        )
        pullbacks.append((pullback, saved))
        node_h = node_next.astype(jnp.bfloat16)
        edge_h = edge_next.astype(jnp.bfloat16)
        node_outs.append(node_h)
        edge_outs.append(edge_h)

    node_back = node_cot.astype(jnp.float32)
    edge_back = edge_cot.astype(jnp.float32)
    node_grads = [None] * len(layers)
    edge_grads = [None] * len(layers)
    grads = [None] * len(layers)
    for layer_index in reversed(range(len(layers))):
        pullback, saved = pullbacks[layer_index]
        node_back, halo_back, edge_back, probe_back = pullback((node_back, edge_back))
        returned = exchange(halo_back.astype(jnp.bfloat16), margin)
        node_back = node_back + jnp.einsum(
            "kn,skd->snd", pick_sent, returned, preferred_element_type=jnp.float32
        )
        node_grads[layer_index] = node_back
        edge_grads[layer_index] = edge_back
        grads[layer_index] = (
            tuple(flatten_rows(value) for value in saved),
            tuple(flatten_rows(value) for value in probe_back),
        )
        if layer_index % 2 == 0:
            pair = grads[layer_index : layer_index + 2]
            reduced = pair_grad_block([entry[0] for entry in pair], [entry[1] for entry in pair])
            grads[layer_index] = reduced[0]
            grads[layer_index + 1] = reduced[1]
    segment_count = lax.axis_size("segment")
    sizes = [
        value.shape[1] // segment_count for value in (edge_w1, edge_w2, node_w1, node_w2, vectors)
    ]
    own = own_layer_grads(grads, sizes)

    def mine(values):
        return lax.dynamic_index_in_dim(jnp.stack(values), segment_index, 0, keepdims=True)

    return (
        mine(node_outs),
        mine(edge_outs),
        mine(node_grads),
        mine(edge_grads),
        own[0],
        own[1],
        own[2],
        own[3],
        own[4],
    )


def solution(mesh):
    in_specs = (
        P("dp", "dom", None),
        P("dp", "dom", None),
        P("dp", "dom", None),
        P("dp", "dom", None),
        P("dom"),
        P("dom"),
        P("dom"),
        P("dom"),
        P("segment", None, None),
        P("segment", None, None),
        P("segment", None, None),
        P("segment", None, None),
        P("segment", None, None),
    )
    out_specs = (
        P("segment", "dp", "dom", None),
        P("segment", "dp", "dom", None),
        P("segment", "dp", "dom", None),
        P("segment", "dp", "dom", None),
        P("segment", None, ("dom", "dp")),
        P("segment", None, ("dom", "dp")),
        P("segment", None, ("dom", "dp")),
        P("segment", None, ("dom", "dp")),
        P("segment", None, ("dom", "dp")),
    )
    return jax.shard_map(local, mesh=mesh, in_specs=in_specs, out_specs=out_specs, check_vma=False)
```

```python
import jax
import jax.numpy as jnp
from jax import lax
from jax.sharding import PartitionSpec as P


def layer_norm(values):
    average = jnp.mean(values, -1, keepdims=True)
    centred = values - average
    return centred * lax.rsqrt(jnp.mean(centred * centred, -1, keepdims=True) + 1e-05)


def layer_local(node_rows, halo_rows, edge_rows, probes, weights, graph_lists):
    edge_w1, edge_w2, node_w1, node_w2, vectors = weights
    sender_row, receiver_row, live_mask = graph_lists
    coeffs = vectors.astype(jnp.float32)
    node_half = node_rows.astype(jnp.bfloat16)
    node_table = jnp.concatenate([node_half, halo_rows.astype(jnp.bfloat16)], 0)
    pick_send = (
        sender_row[:, None] == jnp.arange(node_table.shape[0], dtype=jnp.int32)[None, :]
    ).astype(jnp.bfloat16)
    pick_recv = (
        receiver_row[:, None] == jnp.arange(node_rows.shape[0], dtype=jnp.int32)[None, :]
    ).astype(jnp.bfloat16)
    senders = jnp.dot(pick_send, node_table, preferred_element_type=jnp.float32).astype(
        jnp.bfloat16
    )
    receivers = jnp.dot(pick_recv, node_half, preferred_element_type=jnp.float32).astype(
        jnp.bfloat16
    )
    joined = jnp.concatenate([edge_rows.astype(jnp.bfloat16), senders, receivers], 1)
    edge_pre = jnp.dot(joined, edge_w1, preferred_element_type=jnp.float32) + coeffs[0] + probes[0]
    edge_hid = jax.nn.silu(edge_pre).astype(jnp.bfloat16)
    edge_lin = (
        jnp.dot(edge_hid, edge_w2, preferred_element_type=jnp.float32) + coeffs[1] + probes[1]
    )
    edge_norm = layer_norm(edge_lin)
    message = (edge_norm * coeffs[2] + coeffs[3] + probes[2]) * live_mask[:, None]
    edge_next = edge_rows + message
    incoming = lax.dot_general(
        pick_recv,
        message.astype(jnp.bfloat16),
        (((0,), (0,)), ((), ())),
        preferred_element_type=jnp.float32,
    )
    node_cat = jnp.concatenate([node_half, incoming.astype(jnp.bfloat16)], 1)
    node_pre = (
        jnp.dot(node_cat, node_w1, preferred_element_type=jnp.float32) + coeffs[4] + probes[3]
    )
    node_hid = jax.nn.silu(node_pre).astype(jnp.bfloat16)
    node_lin = (
        jnp.dot(node_hid, node_w2, preferred_element_type=jnp.float32) + coeffs[5] + probes[4]
    )
    node_norm = layer_norm(node_lin)
    node_next = node_rows + node_norm * coeffs[6] + coeffs[7] + probes[5]
    return ((node_next, edge_next), (joined, edge_hid, edge_norm, node_cat, node_hid, node_norm))


def batched_layer(weights, graph_lists):

    def one(node_rows, halo_rows, edge_rows, probes):
        return layer_local(node_rows, halo_rows, edge_rows, probes, weights, graph_lists)

    return jax.vmap(one)


def flatten_rows(buffer):
    return buffer.reshape(-1, buffer.shape[-1])


def exchange(rows, margin):
    count = lax.axis_size("dom")
    from_prev = lax.ppermute(rows[:, margin:], "dom", [(i, (i + 1) % count) for i in range(count)])
    from_next = lax.ppermute(rows[:, :margin], "dom", [((i + 1) % count, i) for i in range(count)])
    return jnp.concatenate([from_prev, from_next], 1)


def gather_weights(params):
    shapes = [value.shape[1:] for value in params]
    packed = jnp.concatenate([value[0] for value in params], 0)
    share_count = lax.axis_size("dp")
    total = packed.shape[0]
    padded_total = -(-total // (8 * share_count)) * (8 * share_count)
    packed = jnp.pad(packed, ((0, padded_total - total), (0, 0)))
    share = padded_total // share_count
    piece = lax.dynamic_slice_in_dim(packed, lax.axis_index("dp") * share, share, 0)
    gathered = lax.all_gather(piece, ("segment", "dp"), axis=0, tiled=False)
    layer_count = gathered.shape[0] // share_count
    gathered = gathered.reshape(layer_count, padded_total, packed.shape[1])
    layers = []
    for layer_index in range(layer_count):
        start = 0
        parts = []
        for shape in shapes:
            parts.append(gathered[layer_index, start : start + shape[0]])
            start += shape[0]
        layers.append(tuple(parts))
    return layers


def layer_grad_block(saved, probe_back):
    segment_count = lax.axis_size("segment")
    segment_index = lax.axis_index("segment")
    joined, edge_hid, edge_norm, node_cat, node_hid, node_norm = saved
    edge_pre_back, edge_lin_back, message_back, node_pre_back, node_lin_back, node_out_back = (
        probe_back
    )
    parts = []
    for left, cotangent in (
        (joined, edge_pre_back),
        (edge_hid, edge_lin_back),
        (node_cat, node_pre_back),
        (node_hid, node_lin_back),
    ):
        size = left.shape[1] // segment_count
        block = lax.dynamic_slice_in_dim(left, segment_index * size, size, 1)
        parts.append(
            lax.dot_general(
                cotangent.astype(jnp.bfloat16),
                block,
                (((0,), (0,)), ((), ())),
                preferred_element_type=jnp.float32,
            )
        )
    vector_back = jnp.stack(
        [
            edge_pre_back.sum(0),
            edge_lin_back.sum(0),
            (message_back * edge_norm).sum(0),
            message_back.sum(0),
            node_pre_back.sum(0),
            node_lin_back.sum(0),
            (node_out_back * node_norm).sum(0),
            node_out_back.sum(0),
        ],
        0,
    )
    size = vector_back.shape[0] // segment_count
    parts.append(lax.dynamic_slice_in_dim(vector_back, segment_index * size, size, 0).T)
    packed = jnp.concatenate(parts, 1)
    reduced = lax.psum_scatter(
        packed.astype(jnp.bfloat16), ("dom", "dp"), scatter_dimension=0, tiled=True
    )
    return reduced.astype(jnp.float32)


def own_layer_grads(reduced, sizes):
    exchanged = lax.all_to_all(jnp.stack(reduced), "segment", 0, 0, tiled=True)
    results = []
    start = 0
    for size in sizes:
        part = jnp.transpose(exchanged[:, :, start : start + size], (0, 2, 1))
        results.append(flatten_rows(part)[None])
        start += size
    return results


def local(
    node_in,
    edge_in,
    node_cot,
    edge_cot,
    send_rows,
    sender_row,
    receiver_row,
    edge_count,
    edge_w1,
    edge_w2,
    node_w1,
    node_w2,
    vectors,
):
    segment_index = lax.axis_index("segment")
    edge_total = edge_in.shape[1]
    margin = send_rows.shape[0] // 2
    live_mask = (jnp.arange(edge_total, dtype=jnp.int32) < edge_count[0]).astype(jnp.float32)
    graph_lists = (sender_row, receiver_row, live_mask)
    layers = gather_weights((edge_w1, edge_w2, node_w1, node_w2, vectors))
    edge_zero = jnp.zeros(edge_in.shape, jnp.float32)
    node_zero = jnp.zeros(node_in.shape, jnp.float32)
    probes = (edge_zero, edge_zero, edge_zero, node_zero, node_zero, node_zero)
    pick_sent = (
        send_rows[:, None] == jnp.arange(node_in.shape[1], dtype=jnp.int32)[None, :]
    ).astype(jnp.bfloat16)

    node_h = node_in
    edge_h = edge_in
    pullbacks = []
    node_outs = []
    edge_outs = []
    for weights in layers:
        halo_h = exchange(jnp.take(node_h, send_rows, axis=1), margin)
        (node_next, edge_next), pullback, saved = jax.vjp(
            batched_layer(weights, graph_lists),
            node_h.astype(jnp.float32),
            halo_h.astype(jnp.float32),
            edge_h.astype(jnp.float32),
            probes,
            has_aux=True,
        )
        pullbacks.append((pullback, saved))
        node_h = node_next.astype(jnp.bfloat16)
        edge_h = edge_next.astype(jnp.bfloat16)
        node_outs.append(node_h)
        edge_outs.append(edge_h)

    node_back = node_cot.astype(jnp.float32)
    edge_back = edge_cot.astype(jnp.float32)
    node_grads = [None] * len(layers)
    edge_grads = [None] * len(layers)
    grads = [None] * len(layers)
    for layer_index in reversed(range(len(layers))):
        pullback, saved = pullbacks[layer_index]
        node_back, halo_back, edge_back, probe_back = pullback((node_back, edge_back))
        returned = exchange(halo_back.astype(jnp.bfloat16), margin)
        node_back = node_back + jnp.einsum(
            "kn,skd->snd", pick_sent, returned, preferred_element_type=jnp.float32
        )
        node_grads[layer_index] = node_back
        edge_grads[layer_index] = edge_back
        grads[layer_index] = layer_grad_block(
            tuple(flatten_rows(value) for value in saved),
            tuple(flatten_rows(value) for value in probe_back),
        )
    segment_count = lax.axis_size("segment")
    sizes = [
        value.shape[1] // segment_count for value in (edge_w1, edge_w2, node_w1, node_w2, vectors)
    ]
    own = own_layer_grads(grads, sizes)

    def mine(values):
        return lax.dynamic_index_in_dim(jnp.stack(values), segment_index, 0, keepdims=True)

    return (
        mine(node_outs),
        mine(edge_outs),
        mine(node_grads),
        mine(edge_grads),
        own[0],
        own[1],
        own[2],
        own[3],
        own[4],
    )


def solution(mesh):
    in_specs = (
        P("dp", "dom", None),
        P("dp", "dom", None),
        P("dp", "dom", None),
        P("dp", "dom", None),
        P("dom"),
        P("dom"),
        P("dom"),
        P("dom"),
        P("segment", None, None),
        P("segment", None, None),
        P("segment", None, None),
        P("segment", None, None),
        P("segment", None, None),
    )
    out_specs = (
        P("segment", "dp", "dom", None),
        P("segment", "dp", "dom", None),
        P("segment", "dp", "dom", None),
        P("segment", "dp", "dom", None),
        P("segment", None, ("dom", "dp")),
        P("segment", None, ("dom", "dp")),
        P("segment", None, ("dom", "dp")),
        P("segment", None, ("dom", "dp")),
        P("segment", None, ("dom", "dp")),
    )
    return jax.shard_map(local, mesh=mesh, in_specs=in_specs, out_specs=out_specs, check_vma=False)
```

```python
import jax
import jax.numpy as jnp
from jax import lax
from jax.sharding import PartitionSpec as P


def layer_norm(values):
    average = jnp.mean(values, -1, keepdims=True)
    centred = values - average
    return centred * lax.rsqrt(jnp.mean(centred * centred, -1, keepdims=True) + 1e-05)


def layer_local(node_rows, halo_rows, edge_rows, probes, weights, graph_lists):
    edge_w1, edge_w2, node_w1, node_w2, vectors = weights
    sender_row, receiver_row, live_mask = graph_lists
    coeffs = vectors.astype(jnp.float32)
    node_half = node_rows.astype(jnp.bfloat16)
    node_table = jnp.concatenate([node_half, halo_rows.astype(jnp.bfloat16)], 0)
    pick_send = (
        sender_row[:, None] == jnp.arange(node_table.shape[0], dtype=jnp.int32)[None, :]
    ).astype(jnp.bfloat16)
    pick_recv = (
        receiver_row[:, None] == jnp.arange(node_rows.shape[0], dtype=jnp.int32)[None, :]
    ).astype(jnp.bfloat16)
    senders = jnp.dot(pick_send, node_table, preferred_element_type=jnp.float32).astype(
        jnp.bfloat16
    )
    receivers = jnp.dot(pick_recv, node_half, preferred_element_type=jnp.float32).astype(
        jnp.bfloat16
    )
    joined = jnp.concatenate([edge_rows.astype(jnp.bfloat16), senders, receivers], 1)
    edge_pre = jnp.dot(joined, edge_w1, preferred_element_type=jnp.float32) + coeffs[0] + probes[0]
    edge_hid = jax.nn.silu(edge_pre).astype(jnp.bfloat16)
    edge_lin = (
        jnp.dot(edge_hid, edge_w2, preferred_element_type=jnp.float32) + coeffs[1] + probes[1]
    )
    edge_norm = layer_norm(edge_lin)
    message = (edge_norm * coeffs[2] + coeffs[3] + probes[2]) * live_mask[:, None]
    edge_next = edge_rows + message
    incoming = lax.dot_general(
        pick_recv,
        message.astype(jnp.bfloat16),
        (((0,), (0,)), ((), ())),
        preferred_element_type=jnp.float32,
    )
    node_cat = jnp.concatenate([node_half, incoming.astype(jnp.bfloat16)], 1)
    node_pre = (
        jnp.dot(node_cat, node_w1, preferred_element_type=jnp.float32) + coeffs[4] + probes[3]
    )
    node_hid = jax.nn.silu(node_pre).astype(jnp.bfloat16)
    node_lin = (
        jnp.dot(node_hid, node_w2, preferred_element_type=jnp.float32) + coeffs[5] + probes[4]
    )
    node_norm = layer_norm(node_lin)
    node_next = node_rows + node_norm * coeffs[6] + coeffs[7] + probes[5]
    return ((node_next, edge_next), (joined, edge_hid, edge_norm, node_cat, node_hid, node_norm))


def batched_layer(weights, graph_lists):

    def one(node_rows, halo_rows, edge_rows, probes):
        return layer_local(node_rows, halo_rows, edge_rows, probes, weights, graph_lists)

    return jax.vmap(one)


def flatten_rows(buffer):
    return buffer.reshape(-1, buffer.shape[-1])


def exchange(rows, margin):
    count = lax.axis_size("dom")
    from_prev = lax.ppermute(rows[:, margin:], "dom", [(i, (i + 1) % count) for i in range(count)])
    from_next = lax.ppermute(rows[:, :margin], "dom", [((i + 1) % count, i) for i in range(count)])
    return jnp.concatenate([from_prev, from_next], 1)


def gather_weights(params):
    shapes = [value.shape[1:] for value in params]
    packed = jnp.concatenate([value[0] for value in params], 0)
    share_count = lax.axis_size("dp")
    total = packed.shape[0]
    padded_total = -(-total // (8 * share_count)) * (8 * share_count)
    packed = jnp.pad(packed, ((0, padded_total - total), (0, 0)))
    share = padded_total // share_count
    piece = lax.dynamic_slice_in_dim(packed, lax.axis_index("dp") * share, share, 0)
    gathered = lax.all_gather(piece, ("segment", "dp"), axis=0, tiled=False)
    layer_count = gathered.shape[0] // share_count
    gathered = gathered.reshape(layer_count, padded_total, packed.shape[1])
    layers = []
    for layer_index in range(layer_count):
        start = 0
        parts = []
        for shape in shapes:
            parts.append(gathered[layer_index, start : start + shape[0]])
            start += shape[0]
        layers.append(tuple(parts))
    return layers


def layer_grad_block(saved, probe_back):
    segment_count = lax.axis_size("segment")
    segment_index = lax.axis_index("segment")
    joined, edge_hid, edge_norm, node_cat, node_hid, node_norm = saved
    edge_pre_back, edge_lin_back, message_back, node_pre_back, node_lin_back, node_out_back = (
        probe_back
    )
    parts = []
    for left, cotangent in (
        (joined, edge_pre_back),
        (edge_hid, edge_lin_back),
        (node_cat, node_pre_back),
        (node_hid, node_lin_back),
    ):
        size = left.shape[1] // segment_count
        block = lax.dynamic_slice_in_dim(left, segment_index * size, size, 1)
        parts.append(
            lax.dot_general(
                cotangent.astype(jnp.bfloat16),
                block,
                (((0,), (0,)), ((), ())),
                preferred_element_type=jnp.float32,
            )
        )
    vector_back = jnp.stack(
        [
            edge_pre_back.sum(0),
            edge_lin_back.sum(0),
            (message_back * edge_norm).sum(0),
            message_back.sum(0),
            node_pre_back.sum(0),
            node_lin_back.sum(0),
            (node_out_back * node_norm).sum(0),
            node_out_back.sum(0),
        ],
        0,
    )
    size = vector_back.shape[0] // segment_count
    parts.append(lax.dynamic_slice_in_dim(vector_back, segment_index * size, size, 0).T)
    return jnp.concatenate(parts, 1)


def reduce_grads(packed):
    reduced = lax.psum_scatter(
        packed.astype(jnp.bfloat16), ("dom", "dp"), scatter_dimension=0, tiled=True
    )
    return reduced


def own_layer_grads(reduced, sizes):
    exchanged = lax.all_to_all(jnp.stack(reduced), "segment", 0, 0, tiled=True)
    results = []
    start = 0
    for size in sizes:
        part = jnp.transpose(exchanged[:, :, start : start + size], (0, 2, 1))
        results.append(flatten_rows(part)[None].astype(jnp.float32))
        start += size
    return results


def local(
    node_in,
    edge_in,
    node_cot,
    edge_cot,
    send_rows,
    sender_row,
    receiver_row,
    edge_count,
    edge_w1,
    edge_w2,
    node_w1,
    node_w2,
    vectors,
):
    segment_index = lax.axis_index("segment")
    edge_total = edge_in.shape[1]
    margin = send_rows.shape[0] // 2
    live_mask = (jnp.arange(edge_total, dtype=jnp.int32) < edge_count[0]).astype(jnp.float32)
    graph_lists = (sender_row, receiver_row, live_mask)
    layers = gather_weights((edge_w1, edge_w2, node_w1, node_w2, vectors))
    edge_zero = jnp.zeros(edge_in.shape, jnp.float32)
    node_zero = jnp.zeros(node_in.shape, jnp.float32)
    probes = (edge_zero, edge_zero, edge_zero, node_zero, node_zero, node_zero)
    pick_sent = (
        send_rows[:, None] == jnp.arange(node_in.shape[1], dtype=jnp.int32)[None, :]
    ).astype(jnp.bfloat16)

    node_h = node_in
    edge_h = edge_in
    pullbacks = []
    node_outs = []
    edge_outs = []
    for weights in layers:
        halo_h = exchange(jnp.take(node_h, send_rows, axis=1), margin)
        (node_next, edge_next), pullback, saved = jax.vjp(
            batched_layer(weights, graph_lists),
            node_h.astype(jnp.float32),
            halo_h.astype(jnp.float32),
            edge_h.astype(jnp.float32),
            probes,
            has_aux=True,
        )
        pullbacks.append((pullback, saved))
        node_h = node_next.astype(jnp.bfloat16)
        edge_h = edge_next.astype(jnp.bfloat16)
        node_outs.append(node_h)
        edge_outs.append(edge_h)

    node_back = node_cot.astype(jnp.float32)
    edge_back = edge_cot.astype(jnp.float32)
    node_grads = [None] * len(layers)
    edge_grads = [None] * len(layers)
    grads = [None] * len(layers)
    for layer_index in reversed(range(len(layers))):
        pullback, saved = pullbacks[layer_index]
        node_back, halo_back, edge_back, probe_back = pullback((node_back, edge_back))
        returned = exchange(halo_back.astype(jnp.bfloat16), margin)
        node_back = node_back + jnp.einsum(
            "kn,skd->snd", pick_sent, returned, preferred_element_type=jnp.float32
        )
        node_grads[layer_index] = node_back
        edge_grads[layer_index] = edge_back
        packed = layer_grad_block(
            tuple(flatten_rows(value) for value in saved),
            tuple(flatten_rows(value) for value in probe_back),
        )
        if layer_index == 0:
            packed, node_grads[0] = lax.optimization_barrier((packed, node_grads[0]))
        grads[layer_index] = reduce_grads(packed)
    segment_count = lax.axis_size("segment")
    sizes = [
        value.shape[1] // segment_count for value in (edge_w1, edge_w2, node_w1, node_w2, vectors)
    ]
    own = own_layer_grads(grads, sizes)

    def mine(values):
        return lax.dynamic_index_in_dim(jnp.stack(values), segment_index, 0, keepdims=True)

    return (
        mine(node_outs),
        mine(edge_outs),
        mine(node_grads),
        mine(edge_grads),
        own[0],
        own[1],
        own[2],
        own[3],
        own[4],
    )


def solution(mesh):
    in_specs = (
        P("dp", "dom", None),
        P("dp", "dom", None),
        P("dp", "dom", None),
        P("dp", "dom", None),
        P("dom"),
        P("dom"),
        P("dom"),
        P("dom"),
        P("segment", None, None),
        P("segment", None, None),
        P("segment", None, None),
        P("segment", None, None),
        P("segment", None, None),
    )
    out_specs = (
        P("segment", "dp", "dom", None),
        P("segment", "dp", "dom", None),
        P("segment", "dp", "dom", None),
        P("segment", "dp", "dom", None),
        P("segment", None, ("dom", "dp")),
        P("segment", None, ("dom", "dp")),
        P("segment", None, ("dom", "dp")),
        P("segment", None, ("dom", "dp")),
        P("segment", None, ("dom", "dp")),
    )
    return jax.shard_map(local, mesh=mesh, in_specs=in_specs, out_specs=out_specs, check_vma=False)
```

```python
import jax
import jax.numpy as jnp
from jax import lax
from jax.sharding import PartitionSpec as P


def layer_norm(values):
    average = jnp.mean(values, -1, keepdims=True)
    centred = values - average
    return centred * lax.rsqrt(jnp.mean(centred * centred, -1, keepdims=True) + 1e-05)


def layer_local(node_rows, halo_rows, edge_rows, probes, weights, graph_lists):
    edge_w1, edge_w2, node_w1, node_w2, vectors = weights
    sender_row, receiver_row, live_mask = graph_lists
    coeffs = vectors.astype(jnp.float32)
    node_half = node_rows.astype(jnp.bfloat16)
    node_table = jnp.concatenate([node_half, halo_rows.astype(jnp.bfloat16)], 0)
    pick_send = (
        sender_row[:, None] == jnp.arange(node_table.shape[0], dtype=jnp.int32)[None, :]
    ).astype(jnp.bfloat16)
    pick_recv = (
        receiver_row[:, None] == jnp.arange(node_rows.shape[0], dtype=jnp.int32)[None, :]
    ).astype(jnp.bfloat16)
    senders = jnp.dot(pick_send, node_table, preferred_element_type=jnp.float32).astype(
        jnp.bfloat16
    )
    receivers = jnp.dot(pick_recv, node_half, preferred_element_type=jnp.float32).astype(
        jnp.bfloat16
    )
    edge_half = edge_rows.astype(jnp.bfloat16)
    joined = jnp.concatenate([edge_half, senders, receivers], 1)
    width = edge_half.shape[1]
    own_part = jnp.dot(
        edge_half, edge_w1[:width], preferred_element_type=jnp.float32
    ) + jnp.dot(receivers, edge_w1[2 * width :], preferred_element_type=jnp.float32)
    edge_pre = (
        own_part
        + jnp.dot(senders, edge_w1[width : 2 * width], preferred_element_type=jnp.float32)
        + coeffs[0]
        + probes[0]
    )
    edge_hid = jax.nn.silu(edge_pre).astype(jnp.bfloat16)
    edge_lin = (
        jnp.dot(edge_hid, edge_w2, preferred_element_type=jnp.float32) + coeffs[1] + probes[1]
    )
    edge_norm = layer_norm(edge_lin)
    message = (edge_norm * coeffs[2] + coeffs[3] + probes[2]) * live_mask[:, None]
    edge_next = edge_rows + message
    incoming = lax.dot_general(
        pick_recv,
        message.astype(jnp.bfloat16),
        (((0,), (0,)), ((), ())),
        preferred_element_type=jnp.float32,
    )
    node_cat = jnp.concatenate([node_half, incoming.astype(jnp.bfloat16)], 1)
    node_pre = (
        jnp.dot(node_cat, node_w1, preferred_element_type=jnp.float32) + coeffs[4] + probes[3]
    )
    node_hid = jax.nn.silu(node_pre).astype(jnp.bfloat16)
    node_lin = (
        jnp.dot(node_hid, node_w2, preferred_element_type=jnp.float32) + coeffs[5] + probes[4]
    )
    node_norm = layer_norm(node_lin)
    node_next = node_rows + node_norm * coeffs[6] + coeffs[7] + probes[5]
    return ((node_next, edge_next), (joined, edge_hid, edge_norm, node_cat, node_hid, node_norm))


def batched_layer(weights, graph_lists):

    def one(node_rows, halo_rows, edge_rows, probes):
        return layer_local(node_rows, halo_rows, edge_rows, probes, weights, graph_lists)

    return jax.vmap(one)


def flatten_rows(buffer):
    return buffer.reshape(-1, buffer.shape[-1])


def exchange(rows, margin):
    count = lax.axis_size("dom")
    from_prev = lax.ppermute(rows[:, margin:], "dom", [(i, (i + 1) % count) for i in range(count)])
    from_next = lax.ppermute(rows[:, :margin], "dom", [((i + 1) % count, i) for i in range(count)])
    return jnp.concatenate([from_prev, from_next], 1)


def gather_weights(params):
    shapes = [value.shape[1:] for value in params]
    packed = jnp.concatenate([value[0] for value in params], 0)
    share_count = lax.axis_size("dp")
    total = packed.shape[0]
    padded_total = -(-total // (8 * share_count)) * (8 * share_count)
    packed = jnp.pad(packed, ((0, padded_total - total), (0, 0)))
    share = padded_total // share_count
    piece = lax.dynamic_slice_in_dim(packed, lax.axis_index("dp") * share, share, 0)
    gathered = lax.all_gather(piece, ("segment", "dp"), axis=0, tiled=False)
    layer_count = gathered.shape[0] // share_count
    gathered = gathered.reshape(layer_count, padded_total, packed.shape[1])
    layers = []
    for layer_index in range(layer_count):
        start = 0
        parts = []
        for shape in shapes:
            parts.append(gathered[layer_index, start : start + shape[0]])
            start += shape[0]
        layers.append(tuple(parts))
    return layers


def layer_grad_block(saved, probe_back):
    segment_count = lax.axis_size("segment")
    segment_index = lax.axis_index("segment")
    joined, edge_hid, edge_norm, node_cat, node_hid, node_norm = saved
    edge_pre_back, edge_lin_back, message_back, node_pre_back, node_lin_back, node_out_back = (
        probe_back
    )
    parts = []
    for left, cotangent in (
        (joined, edge_pre_back),
        (edge_hid, edge_lin_back),
        (node_cat, node_pre_back),
        (node_hid, node_lin_back),
    ):
        size = left.shape[1] // segment_count
        block = lax.dynamic_slice_in_dim(left, segment_index * size, size, 1)
        parts.append(
            lax.dot_general(
                cotangent.astype(jnp.bfloat16),
                block,
                (((0,), (0,)), ((), ())),
                preferred_element_type=jnp.float32,
            )
        )
    vector_back = jnp.stack(
        [
            edge_pre_back.sum(0),
            edge_lin_back.sum(0),
            (message_back * edge_norm).sum(0),
            message_back.sum(0),
            node_pre_back.sum(0),
            node_lin_back.sum(0),
            (node_out_back * node_norm).sum(0),
            node_out_back.sum(0),
        ],
        0,
    )
    size = vector_back.shape[0] // segment_count
    parts.append(lax.dynamic_slice_in_dim(vector_back, segment_index * size, size, 0).T)
    return jnp.concatenate(parts, 1)


def reduce_grads(packed):
    reduced = lax.psum_scatter(
        packed.astype(jnp.bfloat16), ("dom", "dp"), scatter_dimension=0, tiled=True
    )
    return reduced


def own_layer_grads(reduced, sizes):
    exchanged = lax.all_to_all(jnp.stack(reduced), "segment", 0, 0, tiled=True)
    results = []
    start = 0
    for size in sizes:
        part = jnp.transpose(exchanged[:, :, start : start + size], (0, 2, 1))
        results.append(flatten_rows(part)[None].astype(jnp.float32))
        start += size
    return results


def local(
    node_in,
    edge_in,
    node_cot,
    edge_cot,
    send_rows,
    sender_row,
    receiver_row,
    edge_count,
    edge_w1,
    edge_w2,
    node_w1,
    node_w2,
    vectors,
):
    segment_index = lax.axis_index("segment")
    edge_total = edge_in.shape[1]
    margin = send_rows.shape[0] // 2
    live_mask = (jnp.arange(edge_total, dtype=jnp.int32) < edge_count[0]).astype(jnp.float32)
    graph_lists = (sender_row, receiver_row, live_mask)
    layers = gather_weights((edge_w1, edge_w2, node_w1, node_w2, vectors))
    edge_zero = jnp.zeros(edge_in.shape, jnp.float32)
    node_zero = jnp.zeros(node_in.shape, jnp.float32)
    probes = (edge_zero, edge_zero, edge_zero, node_zero, node_zero, node_zero)
    pick_sent = (
        send_rows[:, None] == jnp.arange(node_in.shape[1], dtype=jnp.int32)[None, :]
    ).astype(jnp.bfloat16)

    node_h = node_in
    edge_h = edge_in
    pullbacks = []
    node_outs = []
    edge_outs = []
    for weights in layers:
        halo_h = exchange(jnp.take(node_h, send_rows, axis=1), margin)
        (node_next, edge_next), pullback, saved = jax.vjp(
            batched_layer(weights, graph_lists),
            node_h.astype(jnp.float32),
            halo_h.astype(jnp.float32),
            edge_h.astype(jnp.float32),
            probes,
            has_aux=True,
        )
        pullbacks.append((pullback, saved))
        node_h = node_next.astype(jnp.bfloat16)
        edge_h = edge_next.astype(jnp.bfloat16)
        node_outs.append(node_h)
        edge_outs.append(edge_h)

    node_back = node_cot.astype(jnp.float32)
    edge_back = edge_cot.astype(jnp.float32)
    node_grads = [None] * len(layers)
    edge_grads = [None] * len(layers)
    grads = [None] * len(layers)
    for layer_index in reversed(range(len(layers))):
        pullback, saved = pullbacks[layer_index]
        node_back, halo_back, edge_back, probe_back = pullback((node_back, edge_back))
        returned = exchange(halo_back.astype(jnp.bfloat16), margin)
        node_back = node_back + jnp.einsum(
            "kn,skd->snd", pick_sent, returned, preferred_element_type=jnp.float32
        )
        node_grads[layer_index] = node_back
        edge_grads[layer_index] = edge_back
        packed = layer_grad_block(
            tuple(flatten_rows(value) for value in saved),
            tuple(flatten_rows(value) for value in probe_back),
        )
        if layer_index == 0:
            packed, node_grads[0] = lax.optimization_barrier((packed, node_grads[0]))
        grads[layer_index] = reduce_grads(packed)
    segment_count = lax.axis_size("segment")
    sizes = [
        value.shape[1] // segment_count for value in (edge_w1, edge_w2, node_w1, node_w2, vectors)
    ]
    own = own_layer_grads(grads, sizes)

    def mine(values):
        return lax.dynamic_index_in_dim(jnp.stack(values), segment_index, 0, keepdims=True)

    return (
        mine(node_outs),
        mine(edge_outs),
        mine(node_grads),
        mine(edge_grads),
        own[0],
        own[1],
        own[2],
        own[3],
        own[4],
    )


def solution(mesh):
    in_specs = (
        P("dp", "dom", None),
        P("dp", "dom", None),
        P("dp", "dom", None),
        P("dp", "dom", None),
        P("dom"),
        P("dom"),
        P("dom"),
        P("dom"),
        P("segment", None, None),
        P("segment", None, None),
        P("segment", None, None),
        P("segment", None, None),
        P("segment", None, None),
    )
    out_specs = (
        P("segment", "dp", "dom", None),
        P("segment", "dp", "dom", None),
        P("segment", "dp", "dom", None),
        P("segment", "dp", "dom", None),
        P("segment", None, ("dom", "dp")),
        P("segment", None, ("dom", "dp")),
        P("segment", None, ("dom", "dp")),
        P("segment", None, ("dom", "dp")),
        P("segment", None, ("dom", "dp")),
    )
    return jax.shard_map(local, mesh=mesh, in_specs=in_specs, out_specs=out_specs, check_vma=False)
```

```python
import jax
import jax.numpy as jnp
from jax import lax
from jax.sharding import PartitionSpec as P


def layer_norm(values):
    average = jnp.mean(values, -1, keepdims=True)
    centred = values - average
    return centred * lax.rsqrt(jnp.mean(centred * centred, -1, keepdims=True) + 1e-05)


def layer_local(node_rows, halo_rows, edge_rows, probes, weights, graph_lists):
    edge_w1, edge_w2, node_w1, node_w2, vectors = weights
    sender_row, receiver_row, live_mask = graph_lists
    coeffs = vectors.astype(jnp.float32)
    node_half = node_rows.astype(jnp.bfloat16)
    node_table = jnp.concatenate([node_half, halo_rows.astype(jnp.bfloat16)], 0)
    pick_send = (
        sender_row[:, None] == jnp.arange(node_table.shape[0], dtype=jnp.int32)[None, :]
    ).astype(jnp.bfloat16)
    pick_recv = (
        receiver_row[:, None] == jnp.arange(node_rows.shape[0], dtype=jnp.int32)[None, :]
    ).astype(jnp.bfloat16)
    senders = jnp.dot(pick_send, node_table, preferred_element_type=jnp.float32).astype(
        jnp.bfloat16
    )
    receivers = jnp.dot(pick_recv, node_half, preferred_element_type=jnp.float32).astype(
        jnp.bfloat16
    )
    joined = jnp.concatenate([edge_rows.astype(jnp.bfloat16), senders, receivers], 1)
    edge_pre = jnp.dot(joined, edge_w1, preferred_element_type=jnp.float32) + coeffs[0] + probes[0]
    edge_hid = jax.nn.silu(edge_pre).astype(jnp.bfloat16)
    edge_lin = (
        jnp.dot(edge_hid, edge_w2, preferred_element_type=jnp.float32) + coeffs[1] + probes[1]
    )
    edge_norm = layer_norm(edge_lin)
    message = (edge_norm * coeffs[2] + coeffs[3] + probes[2]) * live_mask[:, None]
    edge_next = edge_rows + message
    incoming = lax.dot_general(
        pick_recv,
        message.astype(jnp.bfloat16),
        (((0,), (0,)), ((), ())),
        preferred_element_type=jnp.float32,
    )
    node_cat = jnp.concatenate([node_half, incoming.astype(jnp.bfloat16)], 1)
    node_pre = (
        jnp.dot(node_cat, node_w1, preferred_element_type=jnp.float32) + coeffs[4] + probes[3]
    )
    node_hid = jax.nn.silu(node_pre).astype(jnp.bfloat16)
    node_lin = (
        jnp.dot(node_hid, node_w2, preferred_element_type=jnp.float32) + coeffs[5] + probes[4]
    )
    node_norm = layer_norm(node_lin)
    node_next = node_rows + node_norm * coeffs[6] + coeffs[7] + probes[5]
    return ((node_next, edge_next), (joined, edge_hid, edge_norm, node_cat, node_hid, node_norm))


def batched_layer(weights, graph_lists):

    def one(node_rows, halo_rows, edge_rows, probes):
        return layer_local(node_rows, halo_rows, edge_rows, probes, weights, graph_lists)

    return jax.vmap(one)


def flatten_rows(buffer):
    return buffer.reshape(-1, buffer.shape[-1])


def exchange(rows, margin):
    count = lax.axis_size("dom")
    from_prev = lax.ppermute(rows[:, margin:], "dom", [(i, (i + 1) % count) for i in range(count)])
    from_next = lax.ppermute(rows[:, :margin], "dom", [((i + 1) % count, i) for i in range(count)])
    return jnp.concatenate([from_prev, from_next], 1)


def gather_weights(params):
    shapes = [value.shape[1:] for value in params]
    packed = jnp.concatenate([value[0] for value in params], 0)
    share_count = lax.axis_size("dp")
    total = packed.shape[0]
    padded_total = -(-total // (8 * share_count)) * (8 * share_count)
    packed = jnp.pad(packed, ((0, padded_total - total), (0, 0)))
    share = padded_total // share_count
    piece = lax.dynamic_slice_in_dim(packed, lax.axis_index("dp") * share, share, 0)
    gathered = lax.all_gather(piece, ("segment", "dp"), axis=0, tiled=False)
    layer_count = gathered.shape[0] // share_count
    gathered = gathered.reshape(layer_count, padded_total, packed.shape[1])
    layers = []
    for layer_index in range(layer_count):
        start = 0
        parts = []
        for shape in shapes:
            parts.append(gathered[layer_index, start : start + shape[0]])
            start += shape[0]
        layers.append(tuple(parts))
    return layers


def layer_grad_block(saved, probe_back):
    segment_count = lax.axis_size("segment")
    segment_index = lax.axis_index("segment")
    joined, edge_hid, edge_norm, node_cat, node_hid, node_norm = saved
    edge_pre_back, edge_lin_back, message_back, node_pre_back, node_lin_back, node_out_back = (
        probe_back
    )
    parts = []
    for left, cotangent in (
        (joined, edge_pre_back),
        (edge_hid, edge_lin_back),
        (node_cat, node_pre_back),
        (node_hid, node_lin_back),
    ):
        size = left.shape[1] // segment_count
        block = lax.dynamic_slice_in_dim(left, segment_index * size, size, 1)
        parts.append(
            lax.dot_general(
                cotangent.astype(jnp.bfloat16),
                block,
                (((0,), (0,)), ((), ())),
                preferred_element_type=jnp.float32,
            )
        )
    vector_back = jnp.stack(
        [
            edge_pre_back.sum(0),
            edge_lin_back.sum(0),
            (message_back * edge_norm).sum(0),
            message_back.sum(0),
            node_pre_back.sum(0),
            node_lin_back.sum(0),
            (node_out_back * node_norm).sum(0),
            node_out_back.sum(0),
        ],
        0,
    )
    size = vector_back.shape[0] // segment_count
    parts.append(lax.dynamic_slice_in_dim(vector_back, segment_index * size, size, 0).T)
    return jnp.concatenate(parts, 1)


def reduce_grads(packed):
    summed = lax.psum(packed.astype(jnp.bfloat16), ("dom", "dp"))
    group = lax.axis_size("dom") * lax.axis_size("dp")
    block = lax.axis_index("dom") * lax.axis_size("dp") + lax.axis_index("dp")
    size = summed.shape[0] // group
    return lax.dynamic_slice_in_dim(summed, block * size, size, 0)


def own_layer_grads(reduced, sizes):
    exchanged = lax.all_to_all(jnp.stack(reduced), "segment", 0, 0, tiled=True)
    results = []
    start = 0
    for size in sizes:
        part = jnp.transpose(exchanged[:, :, start : start + size], (0, 2, 1))
        results.append(flatten_rows(part)[None].astype(jnp.float32))
        start += size
    return results


def local(
    node_in,
    edge_in,
    node_cot,
    edge_cot,
    send_rows,
    sender_row,
    receiver_row,
    edge_count,
    edge_w1,
    edge_w2,
    node_w1,
    node_w2,
    vectors,
):
    segment_index = lax.axis_index("segment")
    edge_total = edge_in.shape[1]
    margin = send_rows.shape[0] // 2
    live_mask = (jnp.arange(edge_total, dtype=jnp.int32) < edge_count[0]).astype(jnp.float32)
    graph_lists = (sender_row, receiver_row, live_mask)
    layers = gather_weights((edge_w1, edge_w2, node_w1, node_w2, vectors))
    edge_zero = jnp.zeros(edge_in.shape, jnp.float32)
    node_zero = jnp.zeros(node_in.shape, jnp.float32)
    probes = (edge_zero, edge_zero, edge_zero, node_zero, node_zero, node_zero)
    pick_sent = (
        send_rows[:, None] == jnp.arange(node_in.shape[1], dtype=jnp.int32)[None, :]
    ).astype(jnp.bfloat16)

    node_h = node_in
    edge_h = edge_in
    pullbacks = []
    node_outs = []
    edge_outs = []
    for weights in layers:
        halo_h = exchange(jnp.take(node_h, send_rows, axis=1), margin)
        (node_next, edge_next), pullback, saved = jax.vjp(
            batched_layer(weights, graph_lists),
            node_h.astype(jnp.float32),
            halo_h.astype(jnp.float32),
            edge_h.astype(jnp.float32),
            probes,
            has_aux=True,
        )
        pullbacks.append((pullback, saved))
        node_h = node_next.astype(jnp.bfloat16)
        edge_h = edge_next.astype(jnp.bfloat16)
        node_outs.append(node_h)
        edge_outs.append(edge_h)

    node_back = node_cot.astype(jnp.float32)
    edge_back = edge_cot.astype(jnp.float32)
    node_grads = [None] * len(layers)
    edge_grads = [None] * len(layers)
    grads = [None] * len(layers)
    for layer_index in reversed(range(len(layers))):
        pullback, saved = pullbacks[layer_index]
        node_back, halo_back, edge_back, probe_back = pullback((node_back, edge_back))
        returned = exchange(halo_back.astype(jnp.bfloat16), margin)
        node_back = node_back + jnp.einsum(
            "kn,skd->snd", pick_sent, returned, preferred_element_type=jnp.float32
        )
        node_grads[layer_index] = node_back
        edge_grads[layer_index] = edge_back
        packed = layer_grad_block(
            tuple(flatten_rows(value) for value in saved),
            tuple(flatten_rows(value) for value in probe_back),
        )
        if layer_index == 0:
            packed, node_grads[0] = lax.optimization_barrier((packed, node_grads[0]))
        grads[layer_index] = reduce_grads(packed)
    segment_count = lax.axis_size("segment")
    sizes = [
        value.shape[1] // segment_count for value in (edge_w1, edge_w2, node_w1, node_w2, vectors)
    ]
    own = own_layer_grads(grads, sizes)

    def mine(values):
        return lax.dynamic_index_in_dim(jnp.stack(values), segment_index, 0, keepdims=True)

    return (
        mine(node_outs),
        mine(edge_outs),
        mine(node_grads),
        mine(edge_grads),
        own[0],
        own[1],
        own[2],
        own[3],
        own[4],
    )


def solution(mesh):
    in_specs = (
        P("dp", "dom", None),
        P("dp", "dom", None),
        P("dp", "dom", None),
        P("dp", "dom", None),
        P("dom"),
        P("dom"),
        P("dom"),
        P("dom"),
        P("segment", None, None),
        P("segment", None, None),
        P("segment", None, None),
        P("segment", None, None),
        P("segment", None, None),
    )
    out_specs = (
        P("segment", "dp", "dom", None),
        P("segment", "dp", "dom", None),
        P("segment", "dp", "dom", None),
        P("segment", "dp", "dom", None),
        P("segment", None, ("dom", "dp")),
        P("segment", None, ("dom", "dp")),
        P("segment", None, ("dom", "dp")),
        P("segment", None, ("dom", "dp")),
        P("segment", None, ("dom", "dp")),
    )
    return jax.shard_map(local, mesh=mesh, in_specs=in_specs, out_specs=out_specs, check_vma=False)
```
